32 devices in a mesh: seq: 4 (over y, x), batch: 8 (over z, core).
Axes of the slice: x: 2, y: 2, z: 4, core: 2. Of those that a mesh axis runs over, the one named last changes fastest.
Arguments:
- feats: bfloat16 [768, 4096], P('seq', 'batch'), parts along dimension 1, may hold values from -6 to 6
- qkv_weight: bfloat16 [768, 2304], replicated, may hold values from -0.21875 to 0.21875
- beta_weight: bfloat16 [768, 6], replicated, may hold values from -0.21875 to 0.21875
- beta_bias: float32 [6], replicated, may hold values from -7 to 0.5
- out_gain: float32 [768], replicated, may hold values from 0.1 to 1.9
Outputs:
- mixed: bfloat16 [4096, 768], P(('batch', 'seq')), parts along dimension 0
The draws below stay inside these ranges and needn't reach their ends.
There are 8 independent parts, one for each index of `batch`. The reference program is written for one: setup_inputs(seed, part) draws one part's arguments, and reference() takes and returns one part's arrays. A program takes and returns all parts, laid end to end along the dimension named above; an argument that names none is the same for every part. Nothing has to cross between parts.
All inputs are finite; a program needn't handle non-finite values.
Results may differ from the reference program's by a relative error of at most 0.012.
Values may be sent and summed in bfloat16 or wider, within the bound.
No kernel may reach another device: no remote copies, remote signals or barrier semaphores. Data moves between devices by JAX's collectives and lax.ppermute only.
A program may use at most 64 MiB of HBM per device.

```python
import jax
import jax.numpy as jnp
from jax import lax

HEADS = 6
HD = 128
GROUP = 64
D = 768
FRAMES = 512


def block_levels(own_key, dims, split, least, high):
    loudness, own = 1.0, jax.random.fold_in(own_key, 6)
    for dim, shards_of in split:
        steps = jnp.exp(jax.random.uniform(jax.random.fold_in(own, dim), (shards_of,), jnp.float32, least / len(split), high / len(split)))
        loudness = loudness * jnp.repeat(steps, dims[dim] // shards_of).reshape([-1 if axis == dim else 1 for axis in range(len(dims))])
    return loudness


def scatter_about(own_key, dims, spread, most, split=(), kind=jnp.bfloat16):
    result = jax.random.normal(own_key, dims, jnp.float32) * spread
    if len(split) > 0:
        result = block_levels(own_key, dims, split, -0.22, 0.18) * result
    return jnp.clip(result, min=-most, max=most).astype(kind)


def setup_inputs(seed: int = 0, part: int = 0) -> dict:
    key_list = jax.random.split(jax.random.key(seed), 6)
    own_keys = jax.random.split(jax.random.fold_in(key_list[5], part), 6)
    feats = scatter_about(own_keys[0], (D, FRAMES), 1.0, 6.0, ((0, 4),))
    qkv_weight = scatter_about(key_list[1], (D, 3 * D), D ** -0.5, 0.21875)
    beta_weight = scatter_about(key_list[2], (D, HEADS), D ** -0.5, 0.21875)
    beta_bias = jnp.clip(jax.random.uniform(key_list[3], (HEADS,), jnp.float32, -7.0, 0.5), -7.0, 0.5)
    out_gain = jnp.clip(1.0 + 0.18 * jax.random.normal(key_list[4], (D,), jnp.float32), 0.1, 1.9)
    return dict(feats=feats, qkv_weight=qkv_weight, beta_weight=beta_weight, beta_bias=beta_bias, out_gain=out_gain)


HIGHEST_ACCURACY = lax.Precision.HIGHEST

def unit_inverse(gram):
    eye_block = jnp.eye(gram.shape[-1], dtype=jnp.float32)
    negated = -jnp.tril(gram, -1)
    inverse = eye_block + negated
    power = negated
    for level in range(5):
        power = jnp.einsum('nhij,nhjk->nhik', power, power, precision=HIGHEST_ACCURACY)
        inverse = inverse + jnp.einsum('nhij,nhjk->nhik', inverse, power, precision=HIGHEST_ACCURACY)
    return inverse

def prepare(qkv, beta):
    rows = qkv.shape[0]
    blocks_count = rows // GROUP
    pieces = qkv.astype(jnp.float32).reshape(rows, 3, HEADS, HD)
    query = pieces[:, 0]
    keys = pieces[:, 1]
    values = pieces[:, 2]
    query = query * lax.rsqrt(lax.optimization_barrier(jnp.sum(query * query, -1, keepdims=True)) + 1e-06)
    keys = keys * lax.rsqrt(lax.optimization_barrier(jnp.sum(keys * keys, -1, keepdims=True)) + 1e-06)

    def blocks(arr):
        return arr.reshape(blocks_count, GROUP, HEADS, arr.shape[-1]).transpose(0, 2, 1, 3)
    query = blocks(query)
    keys = blocks(keys)
    values = blocks(values)
    rates = blocks(beta[:, :, None])
    weighted = keys * rates
    gram = jnp.einsum('nhik,nhjk->nhij', weighted, keys, precision=HIGHEST_ACCURACY)
    inverse = unit_inverse(gram)
    right = jnp.concatenate([weighted, values * rates], -1)
    solved = jnp.einsum('nhij,nhjk->nhik', inverse, right, precision=HIGHEST_ACCURACY)
    wfac = solved[..., :HD]
    ufac = solved[..., HD:]
    scores = jnp.tril(jnp.einsum('nhik,nhjk->nhij', query, keys, precision=HIGHEST_ACCURACY))
    return (query, keys, wfac, ufac, scores)

def finish(outputs, out_gain):
    rows = outputs.shape[0] * GROUP
    flat = outputs.transpose(0, 2, 1, 3).reshape(rows, HEADS, HD)
    power = lax.optimization_barrier(jnp.mean(flat * flat, -1, keepdims=True)) + 1e-06
    normed = flat * lax.rsqrt(power) * out_gain.reshape(HEADS, HD)
    return normed.reshape(rows, HEADS * HD).astype(jnp.bfloat16)

def reference(feats, qkv_weight, beta_weight, beta_bias, out_gain):
    qkv = lax.dot_general(feats, qkv_weight, (((0,), (0,)), ((), ())), preferred_element_type=jnp.float32).astype(jnp.bfloat16)
    logits = lax.dot_general(feats, beta_weight, (((0,), (0,)), ((), ())), preferred_element_type=jnp.float32)
    beta = jax.nn.sigmoid(logits + beta_bias)
    query, keys, wfac, ufac, scores = prepare(qkv, beta)

    def advance(state_matrix, item):
        query_block, key_block, weight_block, update_block, state_block = item
        residual_value = update_block - jnp.einsum('rnf,rfw->rnw', weight_block, state_matrix, precision=HIGHEST_ACCURACY)
        output_rows = jnp.einsum('rnf,rfw->rnw', query_block, state_matrix, precision=HIGHEST_ACCURACY) + jnp.einsum('fco,fop->fcp', state_block, residual_value, precision=HIGHEST_ACCURACY)
        state_matrix = state_matrix + jnp.einsum('mjr,mjz->mrz', key_block, residual_value, precision=HIGHEST_ACCURACY)
        return (state_matrix, output_rows)
    start = jnp.zeros((HEADS, HD, HD), jnp.float32)
    final_state, outputs = lax.scan(advance, start, (query, keys, wfac, ufac, scores))
    return finish(outputs, out_gain)
```

```python
import functools

import jax
import jax.numpy as jnp
from jax import lax
from jax.experimental import pallas as pl
from jax.experimental.pallas import tpu as pltpu
from jax.sharding import PartitionSpec as P

HEADS = 6
HD = 128
GROUP = 64

HIGHEST_ACCURACY = lax.Precision.HIGHEST


def mm(a, b):
    return lax.dot_general(
        a, b, (((1,), (0,)), ((), ())), precision=HIGHEST_ACCURACY,
        preferred_element_type=jnp.float32,
    )


def mm_nt(a, b):
    return lax.dot_general(
        a, b, (((1,), (1,)), ((), ())), precision=HIGHEST_ACCURACY,
        preferred_element_type=jnp.float32,
    )


def mm_tn(a, b):
    return lax.dot_general(
        a, b, (((0,), (0,)), ((), ())), precision=HIGHEST_ACCURACY,
        preferred_element_type=jnp.float32,
    )


def unit_normed(x):
    return x * lax.rsqrt(jnp.sum(x * x, -1, keepdims=True) + 1e-06)


def delta_kernel(qkv_ref, beta_ref, gain_ref, out_ref, state_ref):
    frames = qkv_ref.shape[0]
    width = HEADS * HD
    state_ref[...] = jnp.zeros_like(state_ref)
    row = lax.broadcasted_iota(jnp.int32, (GROUP, GROUP), 0)
    col = lax.broadcasted_iota(jnp.int32, (GROUP, GROUP), 1)
    eye = jnp.where(row == col, 1.0, 0.0).astype(jnp.float32)

    def step(c, carry):
        r0 = pl.multiple_of(c * GROUP, GROUP)
        rows = pl.ds(r0, GROUP)
        for h in range(HEADS):
            query = unit_normed(qkv_ref[rows, pl.ds(h * HD, HD)].astype(jnp.float32))
            keys = unit_normed(qkv_ref[rows, pl.ds(width + h * HD, HD)].astype(jnp.float32))
            values = qkv_ref[rows, pl.ds(2 * width + h * HD, HD)].astype(jnp.float32)
            rates = beta_ref[rows, pl.ds(h, 1)]
            weighted = keys * rates
            gram = mm_nt(weighted, keys)
            negated = jnp.where(row > col, -gram, 0.0)
            inverse = eye + negated
            power = negated
            for level in range(5):
                power = mm(power, power)
                inverse = inverse + mm(inverse, power)
            wfac = mm(inverse, weighted)
            ufac = mm(inverse, values * rates)
            scores = jnp.where(row >= col, mm_nt(query, keys), 0.0)
            state = state_ref[h]
            residual = ufac - mm(wfac, state)
            output = mm(query, state) + mm(scores, residual)
            state_ref[h] = state + mm_tn(keys, residual)
            power_mean = jnp.mean(output * output, -1, keepdims=True) + 1e-06
            gain = gain_ref[:, pl.ds(h * HD, HD)]
            out_ref[rows, pl.ds(h * HD, HD)] = (output * lax.rsqrt(power_mean) * gain).astype(
                out_ref.dtype
            )
        return carry

    lax.fori_loop(0, frames // GROUP, step, 0)


def delta_layer(qkv, beta, gain):
    frames = qkv.shape[0]
    return pl.pallas_call(
        delta_kernel,
        out_shape=jax.ShapeDtypeStruct((frames, HEADS * HD), jnp.bfloat16),
        in_specs=[
            pl.BlockSpec(memory_space=pltpu.VMEM),
            pl.BlockSpec(memory_space=pltpu.VMEM),
            pl.BlockSpec(memory_space=pltpu.VMEM),
        ],
        out_specs=pl.BlockSpec(memory_space=pltpu.VMEM),
        scratch_shapes=[pltpu.VMEM((HEADS, HD, HD), jnp.float32)],
    )(qkv, beta, gain)


def body(feats, qkv_weight, beta_weight, beta_bias, out_gain):
    full = lax.all_gather(feats, "seq", axis=0, tiled=True)
    qkv = lax.dot_general(
        full, qkv_weight, (((0,), (0,)), ((), ())), preferred_element_type=jnp.float32
    ).astype(jnp.bfloat16)
    logits = lax.dot_general(
        full, beta_weight, (((0,), (0,)), ((), ())), preferred_element_type=jnp.float32
    )
    beta = jax.nn.sigmoid(logits + beta_bias)
    mixed = delta_layer(qkv, beta, out_gain.reshape(1, -1))
    count = lax.axis_size("seq")
    mine = lax.axis_index("seq")
    rows = mixed.shape[0] // count
    return lax.dynamic_slice_in_dim(mixed, mine * rows, rows, 0)


def solution(mesh):
    placed = (P("seq", "batch"), P(), P(), P(), P())
    return jax.shard_map(
        body, mesh=mesh, in_specs=placed, out_specs=P(("batch", "seq"), None), check_vma=False
    )
```

```python
import functools

import jax
import jax.numpy as jnp
from jax import lax
from jax.experimental import pallas as pl
from jax.experimental.pallas import tpu as pltpu
from jax.sharding import PartitionSpec as P

HEADS = 6
HD = 128
GROUP = 64

MATMUL_PRECISION = lax.Precision.HIGH


def mm(a, b):
    return lax.dot_general(
        a, b, (((1,), (0,)), ((), ())), precision=MATMUL_PRECISION,
        preferred_element_type=jnp.float32,
    )


def mm_nt(a, b):
    return lax.dot_general(
        a, b, (((1,), (1,)), ((), ())), precision=MATMUL_PRECISION,
        preferred_element_type=jnp.float32,
    )


def mm_tn(a, b):
    return lax.dot_general(
        a, b, (((0,), (0,)), ((), ())), precision=MATMUL_PRECISION,
        preferred_element_type=jnp.float32,
    )


def unit_normed(x):
    return x * lax.rsqrt(jnp.sum(x * x, -1, keepdims=True) + 1e-06)


def delta_kernel(qkv_ref, beta_ref, gain_ref, out_ref, state_ref):
    frames = qkv_ref.shape[0]
    width = HEADS * HD
    state_ref[...] = jnp.zeros_like(state_ref)
    row = lax.broadcasted_iota(jnp.int32, (GROUP, GROUP), 0)
    col = lax.broadcasted_iota(jnp.int32, (GROUP, GROUP), 1)
    eye = jnp.where(row == col, 1.0, 0.0).astype(jnp.float32)

    def step(c, carry):
        r0 = pl.multiple_of(c * GROUP, GROUP)
        rows = pl.ds(r0, GROUP)
        for h in range(HEADS):
            query = unit_normed(qkv_ref[rows, pl.ds(h * HD, HD)].astype(jnp.float32))
            keys = unit_normed(qkv_ref[rows, pl.ds(width + h * HD, HD)].astype(jnp.float32))
            values = qkv_ref[rows, pl.ds(2 * width + h * HD, HD)].astype(jnp.float32)
            rates = beta_ref[rows, pl.ds(h, 1)]
            weighted = keys * rates
            gram = mm_nt(weighted, keys)
            negated = jnp.where(row > col, -gram, 0.0)
            inverse = eye + negated
            power = negated
            for level in range(5):
                power = mm(power, power)
                inverse = inverse + mm(inverse, power)
            wfac = mm(inverse, weighted)
            ufac = mm(inverse, values * rates)
            scores = jnp.where(row >= col, mm_nt(query, keys), 0.0)
            state = state_ref[h]
            residual = ufac - mm(wfac, state)
            output = mm(query, state) + mm(scores, residual)
            state_ref[h] = state + mm_tn(keys, residual)
            power_mean = jnp.mean(output * output, -1, keepdims=True) + 1e-06
            gain = gain_ref[:, pl.ds(h * HD, HD)]
            out_ref[rows, pl.ds(h * HD, HD)] = (output * lax.rsqrt(power_mean) * gain).astype(
                out_ref.dtype
            )
        return carry

    lax.fori_loop(0, frames // GROUP, step, 0)


def delta_layer(qkv, beta, gain):
    frames = qkv.shape[0]
    return pl.pallas_call(
        delta_kernel,
        out_shape=jax.ShapeDtypeStruct((frames, HEADS * HD), jnp.bfloat16),
        in_specs=[
            pl.BlockSpec(memory_space=pltpu.VMEM),
            pl.BlockSpec(memory_space=pltpu.VMEM),
            pl.BlockSpec(memory_space=pltpu.VMEM),
        ],
        out_specs=pl.BlockSpec(memory_space=pltpu.VMEM),
        scratch_shapes=[pltpu.VMEM((HEADS, HD, HD), jnp.float32)],
    )(qkv, beta, gain)


def body(feats, qkv_weight, beta_weight, beta_bias, out_gain):
    full = lax.all_gather(feats, "seq", axis=0, tiled=True)
    qkv = lax.dot_general(
        full, qkv_weight, (((0,), (0,)), ((), ())), preferred_element_type=jnp.float32
    ).astype(jnp.bfloat16)
    logits = lax.dot_general(
        full, beta_weight, (((0,), (0,)), ((), ())), preferred_element_type=jnp.float32
    )
    beta = jax.nn.sigmoid(logits + beta_bias)
    mixed = delta_layer(qkv, beta, out_gain.reshape(1, -1))
    count = lax.axis_size("seq")
    mine = lax.axis_index("seq")
    rows = mixed.shape[0] // count
    return lax.dynamic_slice_in_dim(mixed, mine * rows, rows, 0)


def solution(mesh):
    placed = (P("seq", "batch"), P(), P(), P(), P())
    return jax.shard_map(
        body, mesh=mesh, in_specs=placed, out_specs=P(("batch", "seq"), None), check_vma=False
    )
```

```python
import functools

import jax
import jax.numpy as jnp
from jax import lax
from jax.experimental import pallas as pl
from jax.experimental.pallas import tpu as pltpu
from jax.sharding import PartitionSpec as P

HEADS = 6
HD = 128
GROUP = 64

MATMUL_PRECISION = lax.Precision.HIGH


def mm(a, b):
    return lax.dot_general(
        a, b, (((1,), (0,)), ((), ())), precision=MATMUL_PRECISION,
        preferred_element_type=jnp.float32,
    )


def mm_nt(a, b):
    return lax.dot_general(
        a, b, (((1,), (1,)), ((), ())), precision=MATMUL_PRECISION,
        preferred_element_type=jnp.float32,
    )


def mm_tn(a, b):
    return lax.dot_general(
        a, b, (((0,), (0,)), ((), ())), precision=MATMUL_PRECISION,
        preferred_element_type=jnp.float32,
    )


def unit_normed(x):
    return x * lax.rsqrt(jnp.sum(x * x, -1, keepdims=True) + 1e-06)


def bmm(a, b):
    return lax.dot_general(
        a, b, (((2,), (1,)), ((0,), (0,))), precision=MATMUL_PRECISION,
        preferred_element_type=jnp.float32,
    )


def bmm_nt(a, b):
    return lax.dot_general(
        a, b, (((2,), (2,)), ((0,), (0,))), precision=MATMUL_PRECISION,
        preferred_element_type=jnp.float32,
    )


def delta_kernel(qkv_ref, beta_ref, gain_ref, out_ref, q_ref, k_ref, w_ref, u_ref, p_ref, state_ref):
    frames = qkv_ref.shape[0]
    chunks = frames // GROUP
    width = HEADS * HD
    row = lax.broadcasted_iota(jnp.int32, (chunks, GROUP, GROUP), 1)
    col = lax.broadcasted_iota(jnp.int32, (chunks, GROUP, GROUP), 2)
    eye = jnp.where(row == col, 1.0, 0.0).astype(jnp.float32)

    for h in range(HEADS):
        query = unit_normed(qkv_ref[:, pl.ds(h * HD, HD)].astype(jnp.float32))
        keys = unit_normed(qkv_ref[:, pl.ds(width + h * HD, HD)].astype(jnp.float32))
        values = qkv_ref[:, pl.ds(2 * width + h * HD, HD)].astype(jnp.float32)
        rates = beta_ref[:, pl.ds(h, 1)]
        q_ref[h] = query
        k_ref[h] = keys
        query = query.reshape(chunks, GROUP, HD)
        keys = keys.reshape(chunks, GROUP, HD)
        weighted = (keys.reshape(frames, HD) * rates).reshape(chunks, GROUP, HD)
        scaled = (values * rates).reshape(chunks, GROUP, HD)
        gram = bmm_nt(weighted, keys)
        negated = jnp.where(row > col, -gram, 0.0)
        inverse = eye + negated
        power = negated
        for level in range(5):
            power = bmm(power, power)
            inverse = inverse + bmm(inverse, power)
        w_ref[h] = bmm(inverse, weighted).reshape(frames, HD)
        u_ref[h] = bmm(inverse, scaled).reshape(frames, HD)
        p_ref[h] = jnp.where(row >= col, bmm_nt(query, keys), 0.0).reshape(frames, GROUP)

    state_ref[...] = jnp.zeros_like(state_ref)

    def step(c, carry):
        rows = pl.ds(pl.multiple_of(c * GROUP, GROUP), GROUP)
        for h in range(HEADS):
            state = state_ref[h]
            residual = u_ref[h, rows, :] - mm(w_ref[h, rows, :], state)
            state_ref[h] = state + mm_tn(k_ref[h, rows, :], residual)
            output = mm(q_ref[h, rows, :], state) + mm(p_ref[h, rows, :], residual)
            power_mean = jnp.mean(output * output, -1, keepdims=True) + 1e-06
            gain = gain_ref[:, pl.ds(h * HD, HD)]
            out_ref[rows, pl.ds(h * HD, HD)] = (output * lax.rsqrt(power_mean) * gain).astype(
                out_ref.dtype
            )
        return carry

    lax.fori_loop(0, chunks, step, 0, unroll=chunks <= 8)


def delta_layer(qkv, beta, gain):
    frames = qkv.shape[0]
    return pl.pallas_call(
        delta_kernel,
        out_shape=jax.ShapeDtypeStruct((frames, HEADS * HD), jnp.bfloat16),
        in_specs=[
            pl.BlockSpec(memory_space=pltpu.VMEM),
            pl.BlockSpec(memory_space=pltpu.VMEM),
            pl.BlockSpec(memory_space=pltpu.VMEM),
        ],
        out_specs=pl.BlockSpec(memory_space=pltpu.VMEM),
        scratch_shapes=[
            pltpu.VMEM((HEADS, frames, HD), jnp.float32),
            pltpu.VMEM((HEADS, frames, HD), jnp.float32),
            pltpu.VMEM((HEADS, frames, HD), jnp.float32),
            pltpu.VMEM((HEADS, frames, HD), jnp.float32),
            pltpu.VMEM((HEADS, frames, GROUP), jnp.float32),
            pltpu.VMEM((HEADS, HD, HD), jnp.float32),
        ],
    )(qkv, beta, gain)


def body(feats, qkv_weight, beta_weight, beta_bias, out_gain):
    full = lax.all_gather(feats, "seq", axis=0, tiled=True)
    qkv = lax.dot_general(
        full, qkv_weight, (((0,), (0,)), ((), ())), preferred_element_type=jnp.float32
    ).astype(jnp.bfloat16)
    logits = lax.dot_general(
        full, beta_weight, (((0,), (0,)), ((), ())), preferred_element_type=jnp.float32
    )
    beta = jax.nn.sigmoid(logits + beta_bias)
    mixed = delta_layer(qkv, beta, out_gain.reshape(1, -1))
    count = lax.axis_size("seq")
    mine = lax.axis_index("seq")
    rows = mixed.shape[0] // count
    return lax.dynamic_slice_in_dim(mixed, mine * rows, rows, 0)


def solution(mesh):
    placed = (P("seq", "batch"), P(), P(), P(), P())
    return jax.shard_map(
        body, mesh=mesh, in_specs=placed, out_specs=P(("batch", "seq"), None), check_vma=False
    )
```

```python
import functools

import jax
import jax.numpy as jnp
from jax import lax
from jax.experimental import pallas as pl
from jax.experimental.pallas import tpu as pltpu
from jax.sharding import PartitionSpec as P

HEADS = 6
HD = 128
GROUP = 64

MATMUL_PRECISION = lax.Precision.HIGH


def mm(a, b):
    return lax.dot_general(
        a, b, (((1,), (0,)), ((), ())), precision=MATMUL_PRECISION,
        preferred_element_type=jnp.float32,
    )


def mm_nt(a, b):
    return lax.dot_general(
        a, b, (((1,), (1,)), ((), ())), precision=MATMUL_PRECISION,
        preferred_element_type=jnp.float32,
    )


def mm_tn(a, b):
    return lax.dot_general(
        a, b, (((0,), (0,)), ((), ())), precision=MATMUL_PRECISION,
        preferred_element_type=jnp.float32,
    )


def unit_normed(x):
    return x * lax.rsqrt(jnp.sum(x * x, -1, keepdims=True) + 1e-06)


def bmm(a, b):
    return lax.dot_general(
        a, b, (((2,), (1,)), ((0,), (0,))), precision=MATMUL_PRECISION,
        preferred_element_type=jnp.float32,
    )


def bmm_nt(a, b):
    return lax.dot_general(
        a, b, (((2,), (2,)), ((0,), (0,))), precision=MATMUL_PRECISION,
        preferred_element_type=jnp.float32,
    )


def delta_kernel(qkv_ref, beta_ref, gain_ref, out_ref, q_ref, k_ref, w_ref, u_ref, p_ref, state_ref):
    frames = qkv_ref.shape[0]
    chunks = frames // GROUP
    heads = beta_ref.shape[1]
    width = heads * HD
    row = lax.broadcasted_iota(jnp.int32, (chunks, GROUP, GROUP), 1)
    col = lax.broadcasted_iota(jnp.int32, (chunks, GROUP, GROUP), 2)
    eye = jnp.where(row == col, 1.0, 0.0).astype(jnp.float32)

    for h in range(heads):
        query = unit_normed(qkv_ref[:, pl.ds(h * HD, HD)].astype(jnp.float32))
        keys = unit_normed(qkv_ref[:, pl.ds(width + h * HD, HD)].astype(jnp.float32))
        values = qkv_ref[:, pl.ds(2 * width + h * HD, HD)].astype(jnp.float32)
        rates = beta_ref[:, pl.ds(h, 1)]
        q_ref[h] = query
        k_ref[h] = keys
        query = query.reshape(chunks, GROUP, HD)
        keys = keys.reshape(chunks, GROUP, HD)
        weighted = (keys.reshape(frames, HD) * rates).reshape(chunks, GROUP, HD)
        scaled = (values * rates).reshape(chunks, GROUP, HD)
        gram = bmm_nt(weighted, keys)
        negated = jnp.where(row > col, -gram, 0.0)
        inverse = eye + negated
        power = negated
        for level in range(5):
            power = bmm(power, power)
            inverse = inverse + bmm(inverse, power)
        w_ref[h] = bmm(inverse, weighted).reshape(frames, HD)
        u_ref[h] = bmm(inverse, scaled).reshape(frames, HD)
        p_ref[h] = jnp.where(row >= col, bmm_nt(query, keys), 0.0).reshape(frames, GROUP)

    state_ref[...] = jnp.zeros_like(state_ref)

    def step(c, carry):
        rows = pl.ds(pl.multiple_of(c * GROUP, GROUP), GROUP)
        for h in range(heads):
            state = state_ref[h]
            residual = u_ref[h, rows, :] - mm(w_ref[h, rows, :], state)
            state_ref[h] = state + mm_tn(k_ref[h, rows, :], residual)
            output = mm(q_ref[h, rows, :], state) + mm(p_ref[h, rows, :], residual)
            power_mean = jnp.mean(output * output, -1, keepdims=True) + 1e-06
            gain = gain_ref[:, pl.ds(h * HD, HD)]
            out_ref[rows, pl.ds(h * HD, HD)] = (output * lax.rsqrt(power_mean) * gain).astype(
                out_ref.dtype
            )
        return carry

    lax.fori_loop(0, chunks, step, 0, unroll=chunks <= 8)


def delta_layer(qkv, beta, gain):
    frames, heads = beta.shape
    return pl.pallas_call(
        delta_kernel,
        out_shape=jax.ShapeDtypeStruct((frames, heads * HD), jnp.bfloat16),
        in_specs=[
            pl.BlockSpec(memory_space=pltpu.VMEM),
            pl.BlockSpec(memory_space=pltpu.VMEM),
            pl.BlockSpec(memory_space=pltpu.VMEM),
        ],
        out_specs=pl.BlockSpec(memory_space=pltpu.VMEM),
        scratch_shapes=[
            pltpu.VMEM((heads, frames, HD), jnp.float32),
            pltpu.VMEM((heads, frames, HD), jnp.float32),
            pltpu.VMEM((heads, frames, HD), jnp.float32),
            pltpu.VMEM((heads, frames, HD), jnp.float32),
            pltpu.VMEM((heads, frames, GROUP), jnp.float32),
            pltpu.VMEM((heads, HD, HD), jnp.float32),
        ],
    )(qkv, beta, gain)


def body(feats, qkv_weight, beta_weight, beta_bias, out_gain):
    count = lax.axis_size("seq")
    mine = lax.axis_index("seq")
    slots = -(-HEADS // count)
    heads = jnp.minimum(mine + count * jnp.arange(slots), HEADS - 1)
    full = lax.all_gather(feats, "seq", axis=0, tiled=True)
    channels = qkv_weight.shape[0]
    picked = jnp.take(qkv_weight.reshape(channels, 3, HEADS, HD), heads, axis=2)
    qkv = lax.dot_general(
        full, picked.reshape(channels, 3 * slots * HD), (((0,), (0,)), ((), ())),
        preferred_element_type=jnp.float32,
    ).astype(jnp.bfloat16)
    logits = lax.dot_general(
        full, beta_weight, (((0,), (0,)), ((), ())), preferred_element_type=jnp.float32
    )
    beta = jnp.take(jax.nn.sigmoid(logits + beta_bias), heads, axis=1)
    gain = jnp.take(out_gain.reshape(HEADS, HD), heads, axis=0).reshape(1, slots * HD)
    mixed = delta_layer(qkv, beta, gain)
    frames = mixed.shape[0]
    rows = frames // count
    parts = lax.all_to_all(
        mixed.reshape(count, rows, slots * HD), "seq", split_axis=0, concat_axis=0, tiled=True
    )
    ordered = parts.reshape(count, rows, slots, HD).transpose(1, 2, 0, 3)
    return ordered.reshape(rows, slots * count, HD)[:, :HEADS].reshape(rows, HEADS * HD)


def solution(mesh):
    placed = (P("seq", "batch"), P(), P(), P(), P())
    return jax.shard_map(
        body, mesh=mesh, in_specs=placed, out_specs=P(("batch", "seq"), None), check_vma=False
    )
```

```python
import functools

import jax
import jax.numpy as jnp
from jax import lax
from jax.experimental import pallas as pl
from jax.experimental.pallas import tpu as pltpu
from jax.sharding import PartitionSpec as P

HEADS = 6
HD = 128
GROUP = 64

MATMUL_PRECISION = lax.Precision.HIGH


def mm(a, b):
    return lax.dot_general(
        a, b, (((1,), (0,)), ((), ())), precision=MATMUL_PRECISION,
        preferred_element_type=jnp.float32,
    )


def mm_nt(a, b):
    return lax.dot_general(
        a, b, (((1,), (1,)), ((), ())), precision=MATMUL_PRECISION,
        preferred_element_type=jnp.float32,
    )


def mm_tn(a, b):
    return lax.dot_general(
        a, b, (((0,), (0,)), ((), ())), precision=MATMUL_PRECISION,
        preferred_element_type=jnp.float32,
    )


def unit_normed(x):
    return x * lax.rsqrt(jnp.sum(x * x, -1, keepdims=True) + 1e-06)


def bmm(a, b):
    return lax.dot_general(
        a, b, (((2,), (1,)), ((0,), (0,))), precision=MATMUL_PRECISION,
        preferred_element_type=jnp.float32,
    )


def bmm_nt(a, b):
    return lax.dot_general(
        a, b, (((2,), (2,)), ((0,), (0,))), precision=MATMUL_PRECISION,
        preferred_element_type=jnp.float32,
    )


def delta_kernel(qkv_ref, beta_ref, gain_ref, out_ref, q_ref, k_ref, w_ref, u_ref, p_ref, state_ref):
    frames = qkv_ref.shape[0]
    chunks = frames // GROUP
    heads = beta_ref.shape[1]
    width = heads * HD
    row = lax.broadcasted_iota(jnp.int32, (chunks, GROUP, GROUP), 1)
    col = lax.broadcasted_iota(jnp.int32, (chunks, GROUP, GROUP), 2)
    eye = jnp.where(row == col, 1.0, 0.0).astype(jnp.float32)

    for h in range(heads):
        query = unit_normed(qkv_ref[:, pl.ds(h * HD, HD)].astype(jnp.float32))
        keys = unit_normed(qkv_ref[:, pl.ds(width + h * HD, HD)].astype(jnp.float32))
        values = qkv_ref[:, pl.ds(2 * width + h * HD, HD)].astype(jnp.float32)
        rates = beta_ref[:, pl.ds(h, 1)]
        q_ref[h] = query
        k_ref[h] = keys
        query = query.reshape(chunks, GROUP, HD)
        keys = keys.reshape(chunks, GROUP, HD)
        weighted = (keys.reshape(frames, HD) * rates).reshape(chunks, GROUP, HD)
        scaled = (values * rates).reshape(chunks, GROUP, HD)
        gram = bmm_nt(weighted, keys)
        negated = jnp.where(row > col, -gram, 0.0)
        inverse = eye + negated
        power = negated
        for level in range(5):
            power = bmm(power, power)
            inverse = inverse + bmm(inverse, power)
        w_ref[h] = bmm(inverse, weighted).reshape(frames, HD)
        u_ref[h] = bmm(inverse, scaled).reshape(frames, HD)
        p_ref[h] = jnp.where(row >= col, bmm_nt(query, keys), 0.0).reshape(frames, GROUP)

    state_ref[...] = jnp.zeros_like(state_ref)

    def step(c, carry):
        rows = pl.ds(pl.multiple_of(c * GROUP, GROUP), GROUP)
        for h in range(heads):
            state = state_ref[h]
            residual = u_ref[h, rows, :] - mm(w_ref[h, rows, :], state)
            state_ref[h] = state + mm_tn(k_ref[h, rows, :], residual)
            output = mm(q_ref[h, rows, :], state) + mm(p_ref[h, rows, :], residual)
            power_mean = jnp.mean(output * output, -1, keepdims=True) + 1e-06
            gain = gain_ref[:, pl.ds(h * HD, HD)]
            out_ref[rows, pl.ds(h * HD, HD)] = (output * lax.rsqrt(power_mean) * gain).astype(
                out_ref.dtype
            )
        return carry

    lax.fori_loop(0, chunks, step, 0, unroll=chunks <= 8)


def delta_layer(qkv, beta, gain):
    frames, heads = beta.shape
    return pl.pallas_call(
        delta_kernel,
        out_shape=jax.ShapeDtypeStruct((frames, heads * HD), jnp.bfloat16),
        in_specs=[
            pl.BlockSpec(memory_space=pltpu.VMEM),
            pl.BlockSpec(memory_space=pltpu.VMEM),
            pl.BlockSpec(memory_space=pltpu.VMEM),
        ],
        out_specs=pl.BlockSpec(memory_space=pltpu.VMEM),
        scratch_shapes=[
            pltpu.VMEM((heads, frames, HD), jnp.float32),
            pltpu.VMEM((heads, frames, HD), jnp.float32),
            pltpu.VMEM((heads, frames, HD), jnp.float32),
            pltpu.VMEM((heads, frames, HD), jnp.float32),
            pltpu.VMEM((heads, frames, GROUP), jnp.float32),
            pltpu.VMEM((heads, HD, HD), jnp.float32),
        ],
    )(qkv, beta, gain)


def body(feats, qkv_weight, beta_weight, beta_bias, out_gain):
    count = lax.axis_size("seq")
    mine = lax.axis_index("seq")
    slots = -(-HEADS // count)
    heads = jnp.minimum(mine + count * jnp.arange(slots), HEADS - 1)
    full = lax.all_gather(feats, "seq", axis=0, tiled=True)
    picked = jnp.concatenate(
        [
            lax.dynamic_slice_in_dim(qkv_weight, (part * HEADS + heads[j]) * HD, HD, axis=1)
            for part in range(3)
            for j in range(slots)
        ],
        axis=1,
    )
    qkv = lax.dot_general(
        full, picked, (((0,), (0,)), ((), ())), preferred_element_type=jnp.float32
    ).astype(jnp.bfloat16)
    logits = lax.dot_general(
        full, beta_weight, (((0,), (0,)), ((), ())), preferred_element_type=jnp.float32
    )
    beta = jnp.take(jax.nn.sigmoid(logits + beta_bias), heads, axis=1)
    gain = jnp.take(out_gain.reshape(HEADS, HD), heads, axis=0).reshape(1, slots * HD)
    mixed = delta_layer(qkv, beta, gain)
    frames = mixed.shape[0]
    rows = frames // count
    parts = lax.all_to_all(
        mixed.reshape(count, rows, slots * HD), "seq", split_axis=0, concat_axis=0, tiled=True
    )
    ordered = parts.reshape(count, rows, slots, HD).transpose(1, 2, 0, 3)
    return ordered.reshape(rows, slots * count, HD)[:, :HEADS].reshape(rows, HEADS * HD)


def solution(mesh):
    placed = (P("seq", "batch"), P(), P(), P(), P())
    return jax.shard_map(
        body, mesh=mesh, in_specs=placed, out_specs=P(("batch", "seq"), None), check_vma=False
    )
```

```python
import functools

import jax
import jax.numpy as jnp
from jax import lax
from jax.experimental import pallas as pl
from jax.experimental.pallas import tpu as pltpu
from jax.sharding import PartitionSpec as P

HEADS = 6
HD = 128
GROUP = 64

MATMUL_PRECISION = lax.Precision.HIGH


def mm(a, b):
    return lax.dot_general(
        a, b, (((1,), (0,)), ((), ())), precision=MATMUL_PRECISION,
        preferred_element_type=jnp.float32,
    )


def mm_nt(a, b):
    return lax.dot_general(
        a, b, (((1,), (1,)), ((), ())), precision=MATMUL_PRECISION,
        preferred_element_type=jnp.float32,
    )


def mm_tn(a, b):
    return lax.dot_general(
        a, b, (((0,), (0,)), ((), ())), precision=MATMUL_PRECISION,
        preferred_element_type=jnp.float32,
    )


def unit_normed(x):
    return x * lax.rsqrt(jnp.sum(x * x, -1, keepdims=True) + 1e-06)


def bmm(a, b):
    return lax.dot_general(
        a, b, (((2,), (1,)), ((0,), (0,))), precision=MATMUL_PRECISION,
        preferred_element_type=jnp.float32,
    )


def bmm_nt(a, b):
    return lax.dot_general(
        a, b, (((2,), (2,)), ((0,), (0,))), precision=MATMUL_PRECISION,
        preferred_element_type=jnp.float32,
    )


def delta_kernel(head_ref, feats_ref, *refs):
    slots = (len(refs) - 10) // 4
    weight_refs = refs[: 3 * slots]
    bw_ref, bias_ref = refs[3 * slots], refs[3 * slots + 1]
    gain_refs = refs[3 * slots + 2 : 4 * slots + 2]
    out_ref, qkv_ref, q_ref, k_ref, w_ref, u_ref, p_ref, state_ref = refs[4 * slots + 2 :]
    frames = feats_ref.shape[1]
    chunks = frames // GROUP
    width = slots * HD

    full = feats_ref[...].T
    qkv_ref[...] = jnp.dot(
        full, jnp.concatenate([ref[...] for ref in weight_refs], axis=1),
        preferred_element_type=jnp.float32,
    ).astype(qkv_ref.dtype)
    logits = jnp.dot(full, bw_ref[...], preferred_element_type=jnp.float32) + bias_ref[...]
    beta_all = 1.0 / (1.0 + jnp.exp(-logits))
    lane = lax.broadcasted_iota(jnp.int32, beta_all.shape, 1)

    row = lax.broadcasted_iota(jnp.int32, (chunks, GROUP, GROUP), 1)
    col = lax.broadcasted_iota(jnp.int32, (chunks, GROUP, GROUP), 2)
    eye = jnp.where(row == col, 1.0, 0.0).astype(jnp.float32)

    for h in range(slots):
        query = unit_normed(qkv_ref[:, pl.ds(h * HD, HD)].astype(jnp.float32))
        keys = unit_normed(qkv_ref[:, pl.ds(width + h * HD, HD)].astype(jnp.float32))
        values = qkv_ref[:, pl.ds(2 * width + h * HD, HD)].astype(jnp.float32)
        rates = jnp.sum(jnp.where(lane == head_ref[h], beta_all, 0.0), -1, keepdims=True)
        q_ref[h] = query
        k_ref[h] = keys
        query = query.reshape(chunks, GROUP, HD)
        keys = keys.reshape(chunks, GROUP, HD)
        weighted = (keys.reshape(frames, HD) * rates).reshape(chunks, GROUP, HD)
        scaled = (values * rates).reshape(chunks, GROUP, HD)
        gram = bmm_nt(weighted, keys)
        negated = jnp.where(row > col, -gram, 0.0)
        inverse = eye + negated
        power = negated
        for level in range(5):
            power = bmm(power, power)
            inverse = inverse + bmm(inverse, power)
        w_ref[h] = bmm(inverse, weighted).reshape(frames, HD)
        u_ref[h] = bmm(inverse, scaled).reshape(frames, HD)
        p_ref[h] = jnp.where(row >= col, bmm_nt(query, keys), 0.0).reshape(frames, GROUP)

    state_ref[...] = jnp.zeros_like(state_ref)

    def step(c, carry):
        rows = pl.ds(pl.multiple_of(c * GROUP, GROUP), GROUP)
        for h in range(slots):
            state = state_ref[h]
            residual = u_ref[h, rows, :] - mm(w_ref[h, rows, :], state)
            state_ref[h] = state + mm_tn(k_ref[h, rows, :], residual)
            output = mm(q_ref[h, rows, :], state) + mm(p_ref[h, rows, :], residual)
            power_mean = jnp.mean(output * output, -1, keepdims=True) + 1e-06
            out_ref[rows, pl.ds(h * HD, HD)] = (output * lax.rsqrt(power_mean) * gain_refs[h][0]).astype(
                out_ref.dtype
            )
        return carry

    lax.fori_loop(0, chunks, step, 0, unroll=chunks <= 8)


def delta_layer(heads, full, qkv_weight, beta_weight, beta_bias, out_gain):
    channels, frames = full.shape
    slots = heads.shape[0]
    whole = lambda shape: pl.BlockSpec(shape, lambda i, head: (0,) * len(shape))
    weight_specs = [
        pl.BlockSpec((channels, HD), lambda i, head, p=p, j=j: (0, p * HEADS + head[j]))
        for p in range(3)
        for j in range(slots)
    ]
    gain_specs = [
        pl.BlockSpec((1, 1, HD), lambda i, head, j=j: (head[j], 0, 0)) for j in range(slots)
    ]
    grid_spec = pltpu.PrefetchScalarGridSpec(
        num_scalar_prefetch=1,
        grid=(1,),
        in_specs=[whole((channels, frames))]
        + weight_specs
        + [whole((channels, HEADS)), whole((1, HEADS))]
        + gain_specs,
        out_specs=whole((frames, slots * HD)),
        scratch_shapes=[
            pltpu.VMEM((frames, 3 * slots * HD), jnp.bfloat16),
            pltpu.VMEM((slots, frames, HD), jnp.float32),
            pltpu.VMEM((slots, frames, HD), jnp.float32),
            pltpu.VMEM((slots, frames, HD), jnp.float32),
            pltpu.VMEM((slots, frames, HD), jnp.float32),
            pltpu.VMEM((slots, frames, GROUP), jnp.float32),
            pltpu.VMEM((slots, HD, HD), jnp.float32),
        ],
    )
    gains = out_gain.reshape(HEADS, 1, HD)
    return pl.pallas_call(
        delta_kernel,
        out_shape=jax.ShapeDtypeStruct((frames, slots * HD), jnp.bfloat16),
        grid_spec=grid_spec,
    )(
        heads, full, *([qkv_weight] * (3 * slots)), beta_weight, beta_bias.reshape(1, HEADS),
        *([gains] * slots),
    )


def body(feats, qkv_weight, beta_weight, beta_bias, out_gain):
    count = lax.axis_size("seq")
    mine = lax.axis_index("seq")
    slots = -(-HEADS // count)
    heads = jnp.minimum(mine + count * jnp.arange(slots, dtype=jnp.int32), HEADS - 1)
    full = lax.all_gather(feats, "seq", axis=0, tiled=True)
    mixed = delta_layer(heads, full, qkv_weight, beta_weight, beta_bias, out_gain)
    frames = mixed.shape[0]
    rows = frames // count
    parts = lax.all_to_all(
        mixed.reshape(count, rows, slots * HD), "seq", split_axis=0, concat_axis=0, tiled=True
    )
    ordered = parts.reshape(count, rows, slots, HD).transpose(1, 2, 0, 3)
    return ordered.reshape(rows, slots * count, HD)[:, :HEADS].reshape(rows, HEADS * HD)


def solution(mesh):
    placed = (P("seq", "batch"), P(), P(), P(), P())
    return jax.shard_map(
        body, mesh=mesh, in_specs=placed, out_specs=P(("batch", "seq"), None), check_vma=False
    )
```

```python
import functools

import jax
import jax.numpy as jnp
from jax import lax
from jax.experimental import pallas as pl
from jax.experimental.pallas import tpu as pltpu
from jax.sharding import PartitionSpec as P

HEADS = 6
HD = 128
GROUP = 64

MATMUL_PRECISION = lax.Precision.HIGH


def mm(a, b):
    return lax.dot_general(
        a, b, (((1,), (0,)), ((), ())), precision=MATMUL_PRECISION,
        preferred_element_type=jnp.float32,
    )


def mm_nt(a, b):
    return lax.dot_general(
        a, b, (((1,), (1,)), ((), ())), precision=MATMUL_PRECISION,
        preferred_element_type=jnp.float32,
    )


def mm_tn(a, b):
    return lax.dot_general(
        a, b, (((0,), (0,)), ((), ())), precision=MATMUL_PRECISION,
        preferred_element_type=jnp.float32,
    )


def unit_normed(x):
    return x * lax.rsqrt(jnp.sum(x * x, -1, keepdims=True) + 1e-06)


def bmm(a, b):
    return lax.dot_general(
        a, b, (((2,), (1,)), ((0,), (0,))), precision=MATMUL_PRECISION,
        preferred_element_type=jnp.float32,
    )


def bmm_nt(a, b):
    return lax.dot_general(
        a, b, (((2,), (2,)), ((0,), (0,))), precision=MATMUL_PRECISION,
        preferred_element_type=jnp.float32,
    )


def delta_kernel(head_ref, feats_ref, *refs):
    slots = (len(refs) - 10) // 4
    weight_refs = refs[: 3 * slots]
    bw_ref, bias_ref = refs[3 * slots], refs[3 * slots + 1]
    gain_refs = refs[3 * slots + 2 : 4 * slots + 2]
    out_ref, qkv_ref, q_ref, k_ref, w_ref, u_ref, p_ref, state_ref = refs[4 * slots + 2 :]
    frames = feats_ref.shape[1]
    chunks = frames // GROUP
    width = slots * HD

    full = feats_ref[...].T
    qkv_ref[...] = jnp.dot(
        full, jnp.concatenate([ref[...] for ref in weight_refs], axis=1),
        preferred_element_type=jnp.float32,
    ).astype(qkv_ref.dtype)
    logits = lax.dot_general(
        full, bw_ref[...], (((1,), (1,)), ((), ())), preferred_element_type=jnp.float32
    ) + bias_ref[...]
    beta_all = 1.0 / (1.0 + jnp.exp(-logits))
    lane = lax.broadcasted_iota(jnp.int32, beta_all.shape, 1)

    row = lax.broadcasted_iota(jnp.int32, (chunks, GROUP, GROUP), 1)
    col = lax.broadcasted_iota(jnp.int32, (chunks, GROUP, GROUP), 2)
    eye = jnp.where(row == col, 1.0, 0.0).astype(jnp.float32)

    for h in range(slots):
        query = unit_normed(qkv_ref[:, pl.ds(h * HD, HD)].astype(jnp.float32))
        keys = unit_normed(qkv_ref[:, pl.ds(width + h * HD, HD)].astype(jnp.float32))
        values = qkv_ref[:, pl.ds(2 * width + h * HD, HD)].astype(jnp.float32)
        rates = jnp.sum(jnp.where(lane == head_ref[h], beta_all, 0.0), -1, keepdims=True)
        q_ref[h] = query
        k_ref[h] = keys
        query = query.reshape(chunks, GROUP, HD)
        keys = keys.reshape(chunks, GROUP, HD)
        weighted = (keys.reshape(frames, HD) * rates).reshape(chunks, GROUP, HD)
        scaled = (values * rates).reshape(chunks, GROUP, HD)
        gram = bmm_nt(weighted, keys)
        negated = jnp.where(row > col, -gram, 0.0)
        inverse = eye + negated
        power = negated
        for level in range(5):
            power = bmm(power, power)
            inverse = inverse + bmm(inverse, power)
        w_ref[h] = bmm(inverse, weighted).reshape(frames, HD)
        u_ref[h] = bmm(inverse, scaled).reshape(frames, HD)
        p_ref[h] = jnp.where(row >= col, bmm_nt(query, keys), 0.0).reshape(frames, GROUP)

    state_ref[...] = jnp.zeros_like(state_ref)

    def step(c, carry):
        rows = pl.ds(pl.multiple_of(c * GROUP, GROUP), GROUP)
        for h in range(slots):
            state = state_ref[h]
            residual = u_ref[h, rows, :] - mm(w_ref[h, rows, :], state)
            state_ref[h] = state + mm_tn(k_ref[h, rows, :], residual)
            output = mm(q_ref[h, rows, :], state) + mm(p_ref[h, rows, :], residual)
            power_mean = jnp.mean(output * output, -1, keepdims=True) + 1e-06
            out_ref[rows, pl.ds(h * HD, HD)] = (output * lax.rsqrt(power_mean) * gain_refs[h][...]).astype(
                out_ref.dtype
            )
        return carry

    lax.fori_loop(0, chunks, step, 0, unroll=chunks <= 8)


def delta_layer(heads, full, qkv_weight, beta_weight, beta_bias, out_gain):
    channels, frames = full.shape
    slots = heads.shape[0]
    whole = lambda shape: pl.BlockSpec(shape, lambda i, head: (0,) * len(shape))
    weight_specs = [
        pl.BlockSpec((channels, HD), lambda i, head, p=p, j=j: (0, p * HEADS + head[j]))
        for p in range(3)
        for j in range(slots)
    ]
    gain_specs = [
        pl.BlockSpec((HD,), lambda i, head, j=j: (head[j],)) for j in range(slots)
    ]
    grid_spec = pltpu.PrefetchScalarGridSpec(
        num_scalar_prefetch=1,
        grid=(1,),
        in_specs=[whole((channels, frames))]
        + weight_specs
        + [whole((HEADS, channels)), whole((1, HEADS))]
        + gain_specs,
        out_specs=whole((frames, slots * HD)),
        scratch_shapes=[
            pltpu.VMEM((frames, 3 * slots * HD), jnp.bfloat16),
            pltpu.VMEM((slots, frames, HD), jnp.float32),
            pltpu.VMEM((slots, frames, HD), jnp.float32),
            pltpu.VMEM((slots, frames, HD), jnp.float32),
            pltpu.VMEM((slots, frames, HD), jnp.float32),
            pltpu.VMEM((slots, frames, GROUP), jnp.float32),
            pltpu.VMEM((slots, HD, HD), jnp.float32),
        ],
    )
    gains = out_gain
    return pl.pallas_call(
        delta_kernel,
        out_shape=jax.ShapeDtypeStruct((frames, slots * HD), jnp.bfloat16),
        grid_spec=grid_spec,
    )(
        heads, full, *([qkv_weight] * (3 * slots)), beta_weight.T, beta_bias.reshape(1, HEADS),
        *([gains] * slots),
    )


def body(feats, qkv_weight, beta_weight, beta_bias, out_gain):
    count = lax.axis_size("seq")
    mine = lax.axis_index("seq")
    slots = -(-HEADS // count)
    heads = jnp.minimum(mine * slots + jnp.arange(slots, dtype=jnp.int32), HEADS - 1)
    full = lax.all_gather(feats, "seq", axis=0, tiled=True)
    mixed = delta_layer(heads, full, qkv_weight, beta_weight, beta_bias, out_gain)
    frames = mixed.shape[0]
    rows = frames // count
    parts = lax.all_to_all(mixed, "seq", split_axis=0, concat_axis=1, tiled=True)
    return parts[:, : HEADS * HD]


def solution(mesh):
    placed = (P("seq", "batch"), P(), P(), P(), P())
    return jax.shard_map(
        body, mesh=mesh, in_specs=placed, out_specs=P(("batch", "seq"), None), check_vma=False
    )
```

```python
import functools

import jax
import jax.numpy as jnp
from jax import lax
from jax.experimental import pallas as pl
from jax.experimental.pallas import tpu as pltpu
from jax.sharding import PartitionSpec as P

HEADS = 6
HD = 128
GROUP = 64

MATMUL_PRECISION = lax.Precision.HIGH


def mm(a, b):
    return lax.dot_general(
        a, b, (((1,), (0,)), ((), ())), precision=MATMUL_PRECISION,
        preferred_element_type=jnp.float32,
    )


def mm_nt(a, b):
    return lax.dot_general(
        a, b, (((1,), (1,)), ((), ())), precision=MATMUL_PRECISION,
        preferred_element_type=jnp.float32,
    )


def mm_tn(a, b):
    return lax.dot_general(
        a, b, (((0,), (0,)), ((), ())), precision=MATMUL_PRECISION,
        preferred_element_type=jnp.float32,
    )


def unit_normed(x):
    return x * lax.rsqrt(jnp.sum(x * x, -1, keepdims=True) + 1e-06)


def bmm(a, b):
    return lax.dot_general(
        a, b, (((2,), (1,)), ((0,), (0,))), precision=MATMUL_PRECISION,
        preferred_element_type=jnp.float32,
    )


def bmm_nt(a, b):
    return lax.dot_general(
        a, b, (((2,), (2,)), ((0,), (0,))), precision=MATMUL_PRECISION,
        preferred_element_type=jnp.float32,
    )


def delta_kernel(head_ref, feats_ref, *refs):
    slots = (len(refs) - 9) // 4
    weight_refs = refs[: 3 * slots]
    bw_ref, bias_ref = refs[3 * slots], refs[3 * slots + 1]
    gain_refs = refs[3 * slots + 2 : 4 * slots + 2]
    out_ref, qkv_ref, k_ref, w_ref, u_ref, p_ref, state_ref = refs[4 * slots + 2 :]
    frames = feats_ref.shape[1]
    chunks = frames // GROUP
    width = slots * HD

    full = feats_ref[...].T
    qkv_ref[...] = jnp.dot(
        full, jnp.concatenate([ref[...] for ref in weight_refs], axis=1),
        preferred_element_type=jnp.float32,
    ).astype(qkv_ref.dtype)
    logits = lax.dot_general(
        full, bw_ref[...], (((1,), (1,)), ((), ())), preferred_element_type=jnp.float32
    ) + bias_ref[...]
    beta_all = 1.0 / (1.0 + jnp.exp(-logits))
    lane = lax.broadcasted_iota(jnp.int32, beta_all.shape, 1)

    row = lax.broadcasted_iota(jnp.int32, (chunks, GROUP, GROUP), 1)
    col = lax.broadcasted_iota(jnp.int32, (chunks, GROUP, GROUP), 2)
    eye = jnp.where(row == col, 1.0, 0.0).astype(jnp.float32)

    pairs = chunks // 2
    for h in range(slots):
        query = unit_normed(qkv_ref[:, pl.ds(h * HD, HD)].astype(jnp.float32))
        keys = unit_normed(qkv_ref[:, pl.ds(width + h * HD, HD)].astype(jnp.float32))
        values = qkv_ref[:, pl.ds(2 * width + h * HD, HD)].astype(jnp.float32)
        rates = jnp.sum(jnp.where(lane == head_ref[h], beta_all, 0.0), -1, keepdims=True)
        weighted = (keys * rates).reshape(chunks, GROUP, HD)
        scaled = (values * rates).reshape(chunks, GROUP, HD)
        query = query.reshape(chunks, GROUP, HD)
        keys = keys.reshape(chunks, GROUP, HD)
        gram = bmm_nt(weighted, keys)
        negated = jnp.where(row > col, -gram, 0.0)
        inverse = eye + negated
        power = negated
        for level in range(5):
            power = bmm(power, power)
            inverse = inverse + bmm(inverse, power)
        wfac = bmm(inverse, weighted).reshape(pairs, 2, GROUP, HD)
        ufac = bmm(inverse, scaled).reshape(pairs, 2, GROUP, HD)
        scores = jnp.where(row >= col, bmm_nt(query, keys), 0.0).reshape(pairs, 2, GROUP, GROUP)
        query = query.reshape(pairs, 2, GROUP, HD)
        keys = keys.reshape(pairs, 2, GROUP, HD)
        w1, w2 = wfac[:, 0], wfac[:, 1]
        u1, u2 = ufac[:, 0], ufac[:, 1]
        k1 = keys[:, 0]
        q2 = query[:, 1]
        carry = bmm_nt(w2, k1)
        cross = bmm_nt(q2, k1)
        w_ref[h] = jnp.concatenate([w1, w2 - bmm(carry, w1), query[:, 0], q2], axis=1)
        u_ref[h] = jnp.concatenate([u1, u2 - bmm(carry, u1)], axis=1)
        k_ref[h] = jnp.swapaxes(keys.reshape(pairs, 2 * GROUP, HD), 1, 2)
        zero = jnp.zeros_like(cross)
        p_ref[h] = jnp.concatenate(
            [
                jnp.concatenate([scores[:, 0], zero], axis=2),
                jnp.concatenate([cross, scores[:, 1]], axis=2),
            ],
            axis=1,
        )

    state_ref[...] = jnp.zeros_like(state_ref)
    span = 2 * GROUP

    def step(c, carry):
        rows = pl.ds(pl.multiple_of(c * span, span), span)
        for h in range(slots):
            state = state_ref[h]
            both = mm(w_ref[h, c], state)
            residual = u_ref[h, c] - both[:span]
            state_ref[h] = state + mm(k_ref[h, c], residual)
            output = both[span:] + mm(p_ref[h, c], residual)
            power_mean = jnp.mean(output * output, -1, keepdims=True) + 1e-06
            out_ref[rows, pl.ds(h * HD, HD)] = (output * lax.rsqrt(power_mean) * gain_refs[h][...]).astype(
                out_ref.dtype
            )
        return carry

    lax.fori_loop(0, pairs, step, 0, unroll=pairs <= 8)


def delta_layer(heads, full, qkv_weight, beta_weight, beta_bias, out_gain):
    channels, frames = full.shape
    slots = heads.shape[0]
    whole = lambda shape: pl.BlockSpec(shape, lambda i, head: (0,) * len(shape))
    weight_specs = [
        pl.BlockSpec((channels, HD), lambda i, head, p=p, j=j: (0, p * HEADS + head[j]))
        for p in range(3)
        for j in range(slots)
    ]
    gain_specs = [
        pl.BlockSpec((HD,), lambda i, head, j=j: (head[j],)) for j in range(slots)
    ]
    grid_spec = pltpu.PrefetchScalarGridSpec(
        num_scalar_prefetch=1,
        grid=(1,),
        in_specs=[whole((channels, frames))]
        + weight_specs
        + [whole((HEADS, channels)), whole((1, HEADS))]
        + gain_specs,
        out_specs=whole((frames, slots * HD)),
        scratch_shapes=[
            pltpu.VMEM((frames, 3 * slots * HD), jnp.bfloat16),
            pltpu.VMEM((slots, frames // (2 * GROUP), HD, 2 * GROUP), jnp.float32),
            pltpu.VMEM((slots, frames // (2 * GROUP), 4 * GROUP, HD), jnp.float32),
            pltpu.VMEM((slots, frames // (2 * GROUP), 2 * GROUP, HD), jnp.float32),
            pltpu.VMEM((slots, frames // (2 * GROUP), 2 * GROUP, 2 * GROUP), jnp.float32),
            pltpu.VMEM((slots, HD, HD), jnp.float32),
        ],
    )
    gains = out_gain
    return pl.pallas_call(
        delta_kernel,
        out_shape=jax.ShapeDtypeStruct((frames, slots * HD), jnp.bfloat16),
        grid_spec=grid_spec,
    )(
        heads, full, *([qkv_weight] * (3 * slots)), beta_weight.T, beta_bias.reshape(1, HEADS),
        *([gains] * slots),
    )


def body(feats, qkv_weight, beta_weight, beta_bias, out_gain):
    count = lax.axis_size("seq")
    mine = lax.axis_index("seq")
    slots = -(-HEADS // count)
    heads = jnp.minimum(mine * slots + jnp.arange(slots, dtype=jnp.int32), HEADS - 1)
    full = lax.all_gather(feats, "seq", axis=0, tiled=True)
    mixed = delta_layer(heads, full, qkv_weight, beta_weight, beta_bias, out_gain)
    frames = mixed.shape[0]
    rows = frames // count
    parts = lax.all_to_all(mixed, "seq", split_axis=0, concat_axis=1, tiled=True)
    return parts[:, : HEADS * HD]


def solution(mesh):
    placed = (P("seq", "batch"), P(), P(), P(), P())
    return jax.shard_map(
        body, mesh=mesh, in_specs=placed, out_specs=P(("batch", "seq"), None), check_vma=False
    )
```

```python
import functools

import jax
import jax.numpy as jnp
from jax import lax
from jax.experimental import pallas as pl
from jax.experimental.pallas import tpu as pltpu
from jax.sharding import PartitionSpec as P

HEADS = 6
HD = 128
GROUP = 64

MATMUL_PRECISION = lax.Precision.HIGH


def mm(a, b):
    return lax.dot_general(
        a, b, (((1,), (0,)), ((), ())), precision=MATMUL_PRECISION,
        preferred_element_type=jnp.float32,
    )


def mm_nt(a, b):
    return lax.dot_general(
        a, b, (((1,), (1,)), ((), ())), precision=MATMUL_PRECISION,
        preferred_element_type=jnp.float32,
    )


def mm_tn(a, b):
    return lax.dot_general(
        a, b, (((0,), (0,)), ((), ())), precision=MATMUL_PRECISION,
        preferred_element_type=jnp.float32,
    )


def unit_normed(x):
    return x * lax.rsqrt(jnp.sum(x * x, -1, keepdims=True) + 1e-06)


def bmm(a, b):
    return lax.dot_general(
        a, b, (((2,), (1,)), ((0,), (0,))), precision=MATMUL_PRECISION,
        preferred_element_type=jnp.float32,
    )


def bmm_nt(a, b):
    return lax.dot_general(
        a, b, (((2,), (2,)), ((0,), (0,))), precision=MATMUL_PRECISION,
        preferred_element_type=jnp.float32,
    )


def delta_kernel(head_ref, feats_ref, *refs):
    slots = (len(refs) - 9) // 4
    weight_refs = refs[: 3 * slots]
    bw_ref, bias_ref = refs[3 * slots], refs[3 * slots + 1]
    gain_refs = refs[3 * slots + 2 : 4 * slots + 2]
    out_ref, qkv_ref, k_ref, w_ref, u_ref, p_ref, state_ref = refs[4 * slots + 2 :]
    frames = feats_ref.shape[1]
    chunks = frames // GROUP
    width = slots * HD

    full = feats_ref[...].T
    qkv_ref[...] = jnp.dot(
        full, jnp.concatenate([ref[...] for ref in weight_refs], axis=1),
        preferred_element_type=jnp.float32,
    ).astype(qkv_ref.dtype)
    logits = lax.dot_general(
        full, bw_ref[...], (((1,), (1,)), ((), ())), preferred_element_type=jnp.float32
    ) + bias_ref[...]
    beta_all = 1.0 / (1.0 + jnp.exp(-logits))
    lane = lax.broadcasted_iota(jnp.int32, beta_all.shape, 1)

    row = lax.broadcasted_iota(jnp.int32, (chunks, GROUP, GROUP), 1)
    col = lax.broadcasted_iota(jnp.int32, (chunks, GROUP, GROUP), 2)
    eye = jnp.where(row == col, 1.0, 0.0).astype(jnp.float32)

    pairs = chunks // 2
    for h in range(slots):
        query = unit_normed(qkv_ref[:, pl.ds(h * HD, HD)].astype(jnp.float32))
        keys = unit_normed(qkv_ref[:, pl.ds(width + h * HD, HD)].astype(jnp.float32))
        values = qkv_ref[:, pl.ds(2 * width + h * HD, HD)].astype(jnp.float32)
        rates = jnp.sum(jnp.where(lane == head_ref[h], beta_all, 0.0), -1, keepdims=True)
        weighted = (keys * rates).reshape(chunks, GROUP, HD)
        scaled = (values * rates).reshape(chunks, GROUP, HD)
        query = query.reshape(chunks, GROUP, HD)
        keys = keys.reshape(chunks, GROUP, HD)
        gram = bmm_nt(weighted, keys)
        negated = jnp.where(row > col, -gram, 0.0)
        inverse = eye + negated
        power = negated
        for level in range(5):
            power = bmm(power, power)
            inverse = inverse + bmm(inverse, power)
        wfac = bmm(inverse, weighted).reshape(pairs, 2, GROUP, HD)
        ufac = bmm(inverse, scaled).reshape(pairs, 2, GROUP, HD)
        scores = jnp.where(row >= col, bmm_nt(query, keys), 0.0).reshape(pairs, 2, GROUP, GROUP)
        query = query.reshape(pairs, 2, GROUP, HD)
        keys = keys.reshape(pairs, 2, GROUP, HD)
        w1, w2 = wfac[:, 0], wfac[:, 1]
        u1, u2 = ufac[:, 0], ufac[:, 1]
        k1 = keys[:, 0]
        q2 = query[:, 1]
        carry = bmm_nt(w2, k1)
        cross = bmm_nt(q2, k1)
        w_ref[h] = jnp.concatenate([w1, w2 - bmm(carry, w1), query[:, 0], q2], axis=1)
        u_ref[h] = jnp.concatenate([u1, u2 - bmm(carry, u1)], axis=1)
        k_ref[h] = jnp.swapaxes(keys.reshape(pairs, 2 * GROUP, HD), 1, 2)
        zero = jnp.zeros_like(cross)
        p_ref[h] = jnp.concatenate(
            [
                jnp.concatenate([scores[:, 0], zero], axis=2),
                jnp.concatenate([cross, scores[:, 1]], axis=2),
            ],
            axis=1,
        )

    state_ref[...] = jnp.zeros_like(state_ref)
    span = 2 * GROUP

    def step(c, carry):
        rows = pl.ds(pl.multiple_of(c * span, span), span)
        for h in range(slots):
            state = state_ref[h]
            both = mm(w_ref[h, c], state)
            residual = u_ref[h, c] - both[:span]
            state_ref[h] = state + mm(k_ref[h, c], residual)
            output = both[span:] + mm(p_ref[h, c], residual)
            power_mean = jnp.mean(output * output, -1, keepdims=True) + 1e-06
            out_ref[rows, pl.ds(h * HD, HD)] = (output * lax.rsqrt(power_mean) * gain_refs[h][...]).astype(
                out_ref.dtype
            )
        return carry

    lax.fori_loop(0, pairs, step, 0, unroll=pairs <= 8)


def delta_layer(heads, full, qkv_weight, beta_weight, beta_bias, out_gain):
    channels, frames = full.shape
    slots = heads.shape[0]
    whole = lambda shape: pl.BlockSpec(shape, lambda i, head: (0,) * len(shape))
    weight_specs = [
        pl.BlockSpec((channels, HD), lambda i, head, p=p, j=j: (0, p * HEADS + head[j]))
        for p in range(3)
        for j in range(slots)
    ]
    gain_specs = [
        pl.BlockSpec((HD,), lambda i, head, j=j: (head[j],)) for j in range(slots)
    ]
    grid_spec = pltpu.PrefetchScalarGridSpec(
        num_scalar_prefetch=1,
        grid=(1,),
        in_specs=[whole((channels, frames))]
        + weight_specs
        + [whole((HEADS, channels)), whole((1, HEADS))]
        + gain_specs,
        out_specs=whole((frames, slots * HD)),
        scratch_shapes=[
            pltpu.VMEM((frames, 3 * slots * HD), jnp.bfloat16),
            pltpu.VMEM((slots, frames // (2 * GROUP), HD, 2 * GROUP), jnp.float32),
            pltpu.VMEM((slots, frames // (2 * GROUP), 4 * GROUP, HD), jnp.float32),
            pltpu.VMEM((slots, frames // (2 * GROUP), 2 * GROUP, HD), jnp.float32),
            pltpu.VMEM((slots, frames // (2 * GROUP), 2 * GROUP, 2 * GROUP), jnp.float32),
            pltpu.VMEM((slots, HD, HD), jnp.float32),
        ],
    )
    gains = out_gain
    return pl.pallas_call(
        delta_kernel,
        out_shape=jax.ShapeDtypeStruct((frames, slots * HD), jnp.bfloat16),
        grid_spec=grid_spec,
    )(
        heads, full, *([qkv_weight] * (3 * slots)), beta_weight.T, beta_bias.reshape(1, HEADS),
        *([gains] * slots),
    )


def body(feats, qkv_weight, beta_weight, beta_bias, out_gain):
    count = lax.axis_size("seq")
    mine = lax.axis_index("seq")
    slots = HEADS // 2
    group = mine % 2
    heads = group * slots + jnp.arange(slots, dtype=jnp.int32)
    full = lax.all_gather(feats, "seq", axis=0, tiled=True)
    mixed = delta_layer(heads, full, qkv_weight, beta_weight, beta_bias, out_gain)
    rows = mixed.shape[0] // count
    partner = mine + 1 - 2 * group
    own = lax.dynamic_slice_in_dim(mixed, mine * rows, rows, 0)
    sent = lax.dynamic_slice_in_dim(mixed, partner * rows, rows, 0)
    got = lax.ppermute(sent, "seq", [(s, s + 1 - 2 * (s % 2)) for s in range(count)])
    return jnp.where(
        group == 0, jnp.concatenate([own, got], axis=1), jnp.concatenate([got, own], axis=1)
    )


def solution(mesh):
    placed = (P("seq", "batch"), P(), P(), P(), P())
    return jax.shard_map(
        body, mesh=mesh, in_specs=placed, out_specs=P(("batch", "seq"), None), check_vma=False
    )
```

```python
import functools

import jax
import jax.numpy as jnp
from jax import lax
from jax.experimental import pallas as pl
from jax.experimental.pallas import tpu as pltpu
from jax.sharding import PartitionSpec as P

HEADS = 6
HD = 128
GROUP = 64

MATMUL_PRECISION = lax.Precision.HIGH


def mm(a, b):
    return lax.dot_general(
        a, b, (((1,), (0,)), ((), ())), precision=MATMUL_PRECISION,
        preferred_element_type=jnp.float32,
    )


def mm_nt(a, b):
    return lax.dot_general(
        a, b, (((1,), (1,)), ((), ())), precision=MATMUL_PRECISION,
        preferred_element_type=jnp.float32,
    )


def mm_tn(a, b):
    return lax.dot_general(
        a, b, (((0,), (0,)), ((), ())), precision=MATMUL_PRECISION,
        preferred_element_type=jnp.float32,
    )


def unit_normed(x):
    return x * lax.rsqrt(jnp.sum(x * x, -1, keepdims=True) + 1e-06)


def bmm(a, b):
    return lax.dot_general(
        a, b, (((2,), (1,)), ((0,), (0,))), precision=MATMUL_PRECISION,
        preferred_element_type=jnp.float32,
    )


def bmm_nt(a, b):
    return lax.dot_general(
        a, b, (((2,), (2,)), ((0,), (0,))), precision=MATMUL_PRECISION,
        preferred_element_type=jnp.float32,
    )


def delta_kernel(head_ref, feats_ref, *refs):
    slots = (len(refs) - 10) // 4
    weight_refs = refs[: 3 * slots]
    bw_ref, bias_ref = refs[3 * slots], refs[3 * slots + 1]
    gain_refs = refs[3 * slots + 2 : 4 * slots + 2]
    own_ref, sent_ref, qkv_ref, k_ref, w_ref, u_ref, p_ref, state_ref = refs[4 * slots + 2 :]
    block = own_ref.shape[0]
    frames = feats_ref.shape[1]
    chunks = frames // GROUP
    width = slots * HD

    full = feats_ref[...].T
    qkv_ref[...] = jnp.dot(
        full, jnp.concatenate([ref[...] for ref in weight_refs], axis=1),
        preferred_element_type=jnp.float32,
    ).astype(qkv_ref.dtype)
    logits = lax.dot_general(
        full, bw_ref[...], (((1,), (1,)), ((), ())), preferred_element_type=jnp.float32
    ) + bias_ref[...]
    beta_all = 1.0 / (1.0 + jnp.exp(-logits))
    lane = lax.broadcasted_iota(jnp.int32, beta_all.shape, 1)

    pairs = chunks // 2
    batch = slots * chunks
    row = lax.broadcasted_iota(jnp.int32, (batch, GROUP, GROUP), 1)
    col = lax.broadcasted_iota(jnp.int32, (batch, GROUP, GROUP), 2)
    eye = jnp.where(row == col, 1.0, 0.0).astype(jnp.float32)
    query = jnp.concatenate(
        [unit_normed(qkv_ref[:, pl.ds(h * HD, HD)].astype(jnp.float32)) for h in range(slots)]
    )
    keys = jnp.concatenate(
        [unit_normed(qkv_ref[:, pl.ds(width + h * HD, HD)].astype(jnp.float32)) for h in range(slots)]
    )
    values = jnp.concatenate(
        [qkv_ref[:, pl.ds(2 * width + h * HD, HD)].astype(jnp.float32) for h in range(slots)]
    )
    rates = jnp.concatenate(
        [
            jnp.sum(jnp.where(lane == head_ref[h], beta_all, 0.0), -1, keepdims=True)
            for h in range(slots)
        ]
    )
    weighted = (keys * rates).reshape(batch, GROUP, HD)
    scaled = (values * rates).reshape(batch, GROUP, HD)
    query = query.reshape(batch, GROUP, HD)
    keys = keys.reshape(batch, GROUP, HD)
    gram = bmm_nt(weighted, keys)
    negated = jnp.where(row > col, -gram, 0.0)
    inverse = eye + negated
    power = negated
    for level in range(5):
        power = bmm(power, power)
        inverse = inverse + bmm(inverse, power)
    wfac = bmm(inverse, weighted).reshape(slots * pairs, 2, GROUP, HD)
    ufac = bmm(inverse, scaled).reshape(slots * pairs, 2, GROUP, HD)
    scores = jnp.where(row >= col, bmm_nt(query, keys), 0.0).reshape(slots * pairs, 2, GROUP, GROUP)
    query = query.reshape(slots * pairs, 2, GROUP, HD)
    keys = keys.reshape(slots * pairs, 2, GROUP, HD)
    w1, w2 = wfac[:, 0], wfac[:, 1]
    u1, u2 = ufac[:, 0], ufac[:, 1]
    k1 = keys[:, 0]
    q2 = query[:, 1]
    carry = bmm_nt(w2, k1)
    cross = bmm_nt(q2, k1)
    stacked = jnp.concatenate([w1, w2 - bmm(carry, w1), query[:, 0], q2], axis=1)
    corrected = jnp.concatenate([u1, u2 - bmm(carry, u1)], axis=1)
    flipped = jnp.swapaxes(keys.reshape(slots * pairs, 2 * GROUP, HD), 1, 2)
    zero = jnp.zeros_like(cross)
    blocks = jnp.concatenate(
        [
            jnp.concatenate([scores[:, 0], zero], axis=2),
            jnp.concatenate([cross, scores[:, 1]], axis=2),
        ],
        axis=1,
    )
    for h in range(slots):
        part = slice(h * pairs, (h + 1) * pairs)
        w_ref[h] = stacked[part]
        u_ref[h] = corrected[part]
        k_ref[h] = flipped[part]
        p_ref[h] = blocks[part]

    state_ref[...] = jnp.zeros_like(state_ref)
    span = 2 * GROUP

    def step(c, carry):
        rows = pl.ds(pl.multiple_of(c * span, span), span)
        for h in range(slots):
            state = state_ref[h]
            both = mm(w_ref[h, c], state)
            residual = u_ref[h, c] - both[:span]
            state_ref[h] = state + mm(k_ref[h, c], residual)
            output = both[span:] + mm(p_ref[h, c], residual)
            power_mean = jnp.mean(output * output, -1, keepdims=True) + 1e-06
            mixed = (output * lax.rsqrt(power_mean) * gain_refs[h][...]).astype(own_ref.dtype)
            local = pl.ds(pl.multiple_of((c * span) % block, span), span)

            @pl.when((c * span) // block == head_ref[slots])
            def _():
                own_ref[local, pl.ds(h * HD, HD)] = mixed

            @pl.when((c * span) // block == head_ref[slots + 1])
            def _():
                sent_ref[local, pl.ds(h * HD, HD)] = mixed

        return carry

    lax.fori_loop(0, pairs, step, 0, unroll=pairs <= 8)


def delta_layer(heads, full, qkv_weight, beta_weight, beta_bias, out_gain, block):
    channels, frames = full.shape
    slots = heads.shape[0] - 2
    whole = lambda shape: pl.BlockSpec(shape, lambda i, head: (0,) * len(shape))
    weight_specs = [
        pl.BlockSpec((channels, HD), lambda i, head, p=p, j=j: (0, p * HEADS + head[j]))
        for p in range(3)
        for j in range(slots)
    ]
    gain_specs = [
        pl.BlockSpec((HD,), lambda i, head, j=j: (head[j],)) for j in range(slots)
    ]
    grid_spec = pltpu.PrefetchScalarGridSpec(
        num_scalar_prefetch=1,
        grid=(1,),
        in_specs=[whole((channels, frames))]
        + weight_specs
        + [whole((HEADS, channels)), whole((1, HEADS))]
        + gain_specs,
        out_specs=[whole((block, slots * HD)), whole((block, slots * HD))],
        scratch_shapes=[
            pltpu.VMEM((frames, 3 * slots * HD), jnp.bfloat16),
            pltpu.VMEM((slots, frames // (2 * GROUP), HD, 2 * GROUP), jnp.float32),
            pltpu.VMEM((slots, frames // (2 * GROUP), 4 * GROUP, HD), jnp.float32),
            pltpu.VMEM((slots, frames // (2 * GROUP), 2 * GROUP, HD), jnp.float32),
            pltpu.VMEM((slots, frames // (2 * GROUP), 2 * GROUP, 2 * GROUP), jnp.float32),
            pltpu.VMEM((slots, HD, HD), jnp.float32),
        ],
    )
    gains = out_gain
    return pl.pallas_call(
        delta_kernel,
        out_shape=[
            jax.ShapeDtypeStruct((block, slots * HD), jnp.bfloat16),
            jax.ShapeDtypeStruct((block, slots * HD), jnp.bfloat16),
        ],
        grid_spec=grid_spec,
    )(
        heads, full, *([qkv_weight] * (3 * slots)), beta_weight.T, beta_bias.reshape(1, HEADS),
        *([gains] * slots),
    )


def body(feats, qkv_weight, beta_weight, beta_bias, out_gain):
    count = lax.axis_size("seq")
    mine = lax.axis_index("seq")
    slots = HEADS // 2
    group = mine % 2
    partner = mine + 1 - 2 * group
    meta = jnp.concatenate(
        [group * slots + jnp.arange(slots, dtype=jnp.int32), jnp.stack([mine, partner]).astype(jnp.int32)]
    )
    full = lax.all_gather(feats, "seq", axis=0, tiled=True)
    rows = feats.shape[1] // count
    own, sent = delta_layer(meta, full, qkv_weight, beta_weight, beta_bias, out_gain, rows)
    got = lax.ppermute(sent, "seq", [(s, s + 1 - 2 * (s % 2)) for s in range(count)])
    return jnp.where(
        group == 0, jnp.concatenate([own, got], axis=1), jnp.concatenate([got, own], axis=1)
    )


def solution(mesh):
    placed = (P("seq", "batch"), P(), P(), P(), P())
    return jax.shard_map(
        body, mesh=mesh, in_specs=placed, out_specs=P(("batch", "seq"), None), check_vma=False
    )
```

```python
import functools

import jax
import jax.numpy as jnp
from jax import lax
from jax.experimental import pallas as pl
from jax.experimental.pallas import tpu as pltpu
from jax.sharding import PartitionSpec as P

HEADS = 6
HD = 128
GROUP = 64

MATMUL_PRECISION = lax.Precision.HIGH


def mm(a, b):
    return lax.dot_general(
        a, b, (((1,), (0,)), ((), ())), precision=MATMUL_PRECISION,
        preferred_element_type=jnp.float32,
    )


def mm_nt(a, b):
    return lax.dot_general(
        a, b, (((1,), (1,)), ((), ())), precision=MATMUL_PRECISION,
        preferred_element_type=jnp.float32,
    )


def mm_tn(a, b):
    return lax.dot_general(
        a, b, (((0,), (0,)), ((), ())), precision=MATMUL_PRECISION,
        preferred_element_type=jnp.float32,
    )


def unit_normed(x):
    return x * lax.rsqrt(jnp.sum(x * x, -1, keepdims=True) + 1e-06)


def bmm(a, b):
    return lax.dot_general(
        a, b, (((2,), (1,)), ((0,), (0,))), precision=MATMUL_PRECISION,
        preferred_element_type=jnp.float32,
    )


def bmm_nt(a, b):
    return lax.dot_general(
        a, b, (((2,), (2,)), ((0,), (0,))), precision=MATMUL_PRECISION,
        preferred_element_type=jnp.float32,
    )


def delta_kernel(head_ref, feats_ref, *refs):
    slots = (len(refs) - 9) // 4
    weight_refs = refs[: 3 * slots]
    bw_ref, bias_ref = refs[3 * slots], refs[3 * slots + 1]
    gain_refs = refs[3 * slots + 2 : 4 * slots + 2]
    out_ref, qkv_ref, k_ref, w_ref, u_ref, p_ref, state_ref = refs[4 * slots + 2 :]
    frames = feats_ref.shape[1]
    chunks = frames // GROUP
    width = slots * HD

    full = feats_ref[...].T
    qkv_ref[...] = jnp.dot(
        full, jnp.concatenate([ref[...] for ref in weight_refs], axis=1),
        preferred_element_type=jnp.float32,
    ).astype(qkv_ref.dtype)
    logits = lax.dot_general(
        full, bw_ref[...], (((1,), (1,)), ((), ())), preferred_element_type=jnp.float32
    ) + bias_ref[...]
    beta_all = 1.0 / (1.0 + jnp.exp(-logits))
    lane = lax.broadcasted_iota(jnp.int32, beta_all.shape, 1)

    row = lax.broadcasted_iota(jnp.int32, (chunks, GROUP, GROUP), 1)
    col = lax.broadcasted_iota(jnp.int32, (chunks, GROUP, GROUP), 2)
    eye = jnp.where(row == col, 1.0, 0.0).astype(jnp.float32)

    pairs = chunks // 2
    for h in range(slots):
        query = unit_normed(qkv_ref[:, pl.ds(h * HD, HD)].astype(jnp.float32))
        keys = unit_normed(qkv_ref[:, pl.ds(width + h * HD, HD)].astype(jnp.float32))
        values = qkv_ref[:, pl.ds(2 * width + h * HD, HD)].astype(jnp.float32)
        rates = jnp.sum(jnp.where(lane == head_ref[h], beta_all, 0.0), -1, keepdims=True)
        weighted = (keys * rates).reshape(chunks, GROUP, HD)
        scaled = (values * rates).reshape(chunks, GROUP, HD)
        query = query.reshape(chunks, GROUP, HD)
        keys = keys.reshape(chunks, GROUP, HD)
        gram = bmm_nt(weighted, keys)
        negated = jnp.where(row > col, -gram, 0.0)
        inverse = eye + negated
        power = negated
        for level in range(5):
            power = bmm(power, power)
            inverse = inverse + bmm(inverse, power)
        wfac = bmm(inverse, weighted).reshape(pairs, 2, GROUP, HD)
        ufac = bmm(inverse, scaled).reshape(pairs, 2, GROUP, HD)
        scores = jnp.where(row >= col, bmm_nt(query, keys), 0.0).reshape(pairs, 2, GROUP, GROUP)
        query = query.reshape(pairs, 2, GROUP, HD)
        keys = keys.reshape(pairs, 2, GROUP, HD)
        w1, w2 = wfac[:, 0], wfac[:, 1]
        u1, u2 = ufac[:, 0], ufac[:, 1]
        k1 = keys[:, 0]
        q2 = query[:, 1]
        carry = bmm_nt(w2, k1)
        cross = bmm_nt(q2, k1)
        w_ref[h] = jnp.concatenate([w1, w2 - bmm(carry, w1), query[:, 0], q2], axis=1)
        u_ref[h] = jnp.concatenate([u1, u2 - bmm(carry, u1)], axis=1)
        k_ref[h] = jnp.swapaxes(keys.reshape(pairs, 2 * GROUP, HD), 1, 2)
        zero = jnp.zeros_like(cross)
        p_ref[h] = jnp.concatenate(
            [
                jnp.concatenate([scores[:, 0], zero], axis=2),
                jnp.concatenate([cross, scores[:, 1]], axis=2),
            ],
            axis=1,
        )

    state_ref[...] = jnp.zeros_like(state_ref)
    span = 2 * GROUP

    def step(c, carry):
        rows = pl.ds(pl.multiple_of(c * span, span), span)
        for h in range(slots):
            state = state_ref[h]
            both = mm(w_ref[h, c], state)
            residual = u_ref[h, c] - both[:span]
            state_ref[h] = state + mm(k_ref[h, c], residual)
            output = both[span:] + mm(p_ref[h, c], residual)
            power_mean = jnp.mean(output * output, -1, keepdims=True) + 1e-06
            out_ref[rows, pl.ds(h * HD, HD)] = (output * lax.rsqrt(power_mean) * gain_refs[h][...]).astype(
                out_ref.dtype
            )
        return carry

    lax.fori_loop(0, pairs, step, 0, unroll=pairs <= 8)


def delta_layer(heads, full, qkv_weight, beta_weight, beta_bias, out_gain):
    channels, frames = full.shape
    slots = heads.shape[0]
    whole = lambda shape: pl.BlockSpec(shape, lambda i, head: (0,) * len(shape))
    weight_specs = [
        pl.BlockSpec((channels, HD), lambda i, head, p=p, j=j: (0, p * HEADS + head[j]))
        for p in range(3)
        for j in range(slots)
    ]
    gain_specs = [
        pl.BlockSpec((HD,), lambda i, head, j=j: (head[j],)) for j in range(slots)
    ]
    grid_spec = pltpu.PrefetchScalarGridSpec(
        num_scalar_prefetch=1,
        grid=(1,),
        in_specs=[whole((channels, frames))]
        + weight_specs
        + [whole((HEADS, channels)), whole((1, HEADS))]
        + gain_specs,
        out_specs=whole((frames, slots * HD)),
        scratch_shapes=[
            pltpu.VMEM((frames, 3 * slots * HD), jnp.bfloat16),
            pltpu.VMEM((slots, frames // (2 * GROUP), HD, 2 * GROUP), jnp.float32),
            pltpu.VMEM((slots, frames // (2 * GROUP), 4 * GROUP, HD), jnp.float32),
            pltpu.VMEM((slots, frames // (2 * GROUP), 2 * GROUP, HD), jnp.float32),
            pltpu.VMEM((slots, frames // (2 * GROUP), 2 * GROUP, 2 * GROUP), jnp.float32),
            pltpu.VMEM((slots, HD, HD), jnp.float32),
        ],
    )
    gains = out_gain
    return pl.pallas_call(
        delta_kernel,
        out_shape=jax.ShapeDtypeStruct((frames, slots * HD), jnp.bfloat16),
        grid_spec=grid_spec,
    )(
        heads, full, *([qkv_weight] * (3 * slots)), beta_weight.T, beta_bias.reshape(1, HEADS),
        *([gains] * slots),
    )


def body(feats, qkv_weight, beta_weight, beta_bias, out_gain):
    count = lax.axis_size("seq")
    mine = lax.axis_index("seq")
    slots = -(-HEADS // count)
    heads = jnp.minimum(mine * slots + jnp.arange(slots, dtype=jnp.int32), HEADS - 1)
    full = lax.all_gather(feats, "seq", axis=0, tiled=True)
    mixed = delta_layer(heads, full, qkv_weight, beta_weight, beta_bias, out_gain)
    frames = mixed.shape[0]
    rows = frames // count
    blocks = mixed.reshape(count, rows, slots * HD)
    got = [lax.dynamic_index_in_dim(blocks, mine, 0, keepdims=False)]
    for d in range(1, count):
        part = lax.dynamic_index_in_dim(blocks, (mine + d) % count, 0, keepdims=False)
        got.append(lax.ppermute(part, "seq", [(s, (s + d) % count) for s in range(count)]))
    needed = -(-HEADS // slots)
    placed = []
    for k in range(needed):
        pick = got[0]
        for d in range(1, count):
            pick = jnp.where((mine - d) % count == k, got[d], pick)
        placed.append(pick)
    return jnp.concatenate(placed, axis=1)[:, : HEADS * HD]


def solution(mesh):
    placed = (P("seq", "batch"), P(), P(), P(), P())
    return jax.shard_map(
        body, mesh=mesh, in_specs=placed, out_specs=P(("batch", "seq"), None), check_vma=False
    )
```

```python
import functools

import jax
import jax.numpy as jnp
from jax import lax
from jax.experimental import pallas as pl
from jax.experimental.pallas import tpu as pltpu
from jax.sharding import PartitionSpec as P

HEADS = 6
HD = 128
GROUP = 64

MATMUL_PRECISION = lax.Precision.HIGH


def mm(a, b):
    return lax.dot_general(
        a, b, (((1,), (0,)), ((), ())), precision=MATMUL_PRECISION,
        preferred_element_type=jnp.float32,
    )


def mm_nt(a, b):
    return lax.dot_general(
        a, b, (((1,), (1,)), ((), ())), precision=MATMUL_PRECISION,
        preferred_element_type=jnp.float32,
    )


def mm_tn(a, b):
    return lax.dot_general(
        a, b, (((0,), (0,)), ((), ())), precision=MATMUL_PRECISION,
        preferred_element_type=jnp.float32,
    )


def unit_normed(x):
    return x * lax.rsqrt(jnp.sum(x * x, -1, keepdims=True) + 1e-06)


def bmm(a, b):
    return lax.dot_general(
        a, b, (((2,), (1,)), ((0,), (0,))), precision=MATMUL_PRECISION,
        preferred_element_type=jnp.float32,
    )


def bmm_nt(a, b):
    return lax.dot_general(
        a, b, (((2,), (2,)), ((0,), (0,))), precision=MATMUL_PRECISION,
        preferred_element_type=jnp.float32,
    )


def delta_kernel(count, head_ref, feats_ref, *refs):
    slots = (len(refs) - 9) // 4
    weight_refs = refs[: 3 * slots]
    bw_ref, bias_ref = refs[3 * slots], refs[3 * slots + 1]
    gain_refs = refs[3 * slots + 2 : 4 * slots + 2]
    out_ref, qkv_ref, k_ref, w_ref, u_ref, p_ref, state_ref = refs[4 * slots + 2 :]
    frames = feats_ref.shape[1]
    chunks = frames // GROUP
    width = slots * HD

    full = feats_ref[...].T
    qkv_ref[...] = jnp.dot(
        full, jnp.concatenate([ref[...] for ref in weight_refs], axis=1),
        preferred_element_type=jnp.float32,
    ).astype(qkv_ref.dtype)
    logits = lax.dot_general(
        full, bw_ref[...], (((1,), (1,)), ((), ())), preferred_element_type=jnp.float32
    ) + bias_ref[...]
    beta_all = 1.0 / (1.0 + jnp.exp(-logits))
    lane = lax.broadcasted_iota(jnp.int32, beta_all.shape, 1)

    row = lax.broadcasted_iota(jnp.int32, (chunks, GROUP, GROUP), 1)
    col = lax.broadcasted_iota(jnp.int32, (chunks, GROUP, GROUP), 2)
    eye = jnp.where(row == col, 1.0, 0.0).astype(jnp.float32)

    pairs = chunks // 2
    for h in range(slots):
        query = unit_normed(qkv_ref[:, pl.ds(h * HD, HD)].astype(jnp.float32))
        keys = unit_normed(qkv_ref[:, pl.ds(width + h * HD, HD)].astype(jnp.float32))
        values = qkv_ref[:, pl.ds(2 * width + h * HD, HD)].astype(jnp.float32)
        rates = jnp.sum(jnp.where(lane == head_ref[h], beta_all, 0.0), -1, keepdims=True)
        weighted = (keys * rates).reshape(chunks, GROUP, HD)
        scaled = (values * rates).reshape(chunks, GROUP, HD)
        query = query.reshape(chunks, GROUP, HD)
        keys = keys.reshape(chunks, GROUP, HD)
        gram = bmm_nt(weighted, keys)
        negated = jnp.where(row > col, -gram, 0.0)
        inverse = eye + negated
        power = negated
        for level in range(5):
            power = bmm(power, power)
            inverse = inverse + bmm(inverse, power)
        wfac = bmm(inverse, weighted).reshape(pairs, 2, GROUP, HD)
        ufac = bmm(inverse, scaled).reshape(pairs, 2, GROUP, HD)
        scores = jnp.where(row >= col, bmm_nt(query, keys), 0.0).reshape(pairs, 2, GROUP, GROUP)
        query = query.reshape(pairs, 2, GROUP, HD)
        keys = keys.reshape(pairs, 2, GROUP, HD)
        w1, w2 = wfac[:, 0], wfac[:, 1]
        u1, u2 = ufac[:, 0], ufac[:, 1]
        k1 = keys[:, 0]
        q2 = query[:, 1]
        carry = bmm_nt(w2, k1)
        cross = bmm_nt(q2, k1)
        w_ref[h] = jnp.concatenate([w1, w2 - bmm(carry, w1), query[:, 0], q2], axis=1)
        u_ref[h] = jnp.concatenate([u1, u2 - bmm(carry, u1)], axis=1)
        k_ref[h] = jnp.swapaxes(keys.reshape(pairs, 2 * GROUP, HD), 1, 2)
        zero = jnp.zeros_like(cross)
        p_ref[h] = jnp.concatenate(
            [
                jnp.concatenate([scores[:, 0], zero], axis=2),
                jnp.concatenate([cross, scores[:, 1]], axis=2),
            ],
            axis=1,
        )

    state_ref[...] = jnp.zeros_like(state_ref)
    span = 2 * GROUP

    def step(c, carry):
        block = frames // count
        owner = ((c * span) // block - head_ref[slots] + count) % count
        place = pl.ds(pl.multiple_of(owner * block + (c * span) % block, span), span)
        for h in range(slots):
            state = state_ref[h]
            both = mm(w_ref[h, c], state)
            residual = u_ref[h, c] - both[:span]
            state_ref[h] = state + mm(k_ref[h, c], residual)
            output = both[span:] + mm(p_ref[h, c], residual)
            power_mean = jnp.mean(output * output, -1, keepdims=True) + 1e-06
            out_ref[place, pl.ds(h * HD, HD)] = (output * lax.rsqrt(power_mean) * gain_refs[h][...]).astype(
                out_ref.dtype
            )
        return carry

    lax.fori_loop(0, pairs, step, 0, unroll=pairs <= 8)


def delta_layer(heads, full, qkv_weight, beta_weight, beta_bias, out_gain, count):
    channels, frames = full.shape
    slots = heads.shape[0] - 1
    whole = lambda shape: pl.BlockSpec(shape, lambda i, head: (0,) * len(shape))
    weight_specs = [
        pl.BlockSpec((channels, HD), lambda i, head, p=p, j=j: (0, p * HEADS + head[j]))
        for p in range(3)
        for j in range(slots)
    ]
    gain_specs = [
        pl.BlockSpec((HD,), lambda i, head, j=j: (head[j],)) for j in range(slots)
    ]
    grid_spec = pltpu.PrefetchScalarGridSpec(
        num_scalar_prefetch=1,
        grid=(1,),
        in_specs=[whole((channels, frames))]
        + weight_specs
        + [whole((HEADS, channels)), whole((1, HEADS))]
        + gain_specs,
        out_specs=whole((frames, slots * HD)),
        scratch_shapes=[
            pltpu.VMEM((frames, 3 * slots * HD), jnp.bfloat16),
            pltpu.VMEM((slots, frames // (2 * GROUP), HD, 2 * GROUP), jnp.float32),
            pltpu.VMEM((slots, frames // (2 * GROUP), 4 * GROUP, HD), jnp.float32),
            pltpu.VMEM((slots, frames // (2 * GROUP), 2 * GROUP, HD), jnp.float32),
            pltpu.VMEM((slots, frames // (2 * GROUP), 2 * GROUP, 2 * GROUP), jnp.float32),
            pltpu.VMEM((slots, HD, HD), jnp.float32),
        ],
    )
    gains = out_gain
    return pl.pallas_call(
        functools.partial(delta_kernel, count),
        out_shape=jax.ShapeDtypeStruct((frames, slots * HD), jnp.bfloat16),
        grid_spec=grid_spec,
    )(
        heads, full, *([qkv_weight] * (3 * slots)), beta_weight.T, beta_bias.reshape(1, HEADS),
        *([gains] * slots),
    )


def body(feats, qkv_weight, beta_weight, beta_bias, out_gain):
    count = lax.axis_size("seq")
    mine = lax.axis_index("seq")
    slots = -(-HEADS // count)
    heads = jnp.minimum(mine * slots + jnp.arange(slots, dtype=jnp.int32), HEADS - 1)
    meta = jnp.concatenate([heads, mine.astype(jnp.int32).reshape(1)])
    full = lax.all_gather(feats, "seq", axis=0, tiled=True)
    mixed = delta_layer(meta, full, qkv_weight, beta_weight, beta_bias, out_gain, count)
    frames = mixed.shape[0]
    rows = frames // count
    blocks = mixed.reshape(count, rows, slots * HD)
    got = [blocks[0]]
    for d in range(1, count):
        got.append(lax.ppermute(blocks[d], "seq", [(s, (s + d) % count) for s in range(count)]))
    needed = -(-HEADS // slots)
    placed = []
    for k in range(needed):
        pick = got[0]
        for d in range(1, count):
            pick = jnp.where((mine - d) % count == k, got[d], pick)
        placed.append(pick)
    return jnp.concatenate(placed, axis=1)[:, : HEADS * HD]


def solution(mesh):
    placed = (P("seq", "batch"), P(), P(), P(), P())
    return jax.shard_map(
        body, mesh=mesh, in_specs=placed, out_specs=P(("batch", "seq"), None), check_vma=False
    )
```

```python
import functools

import jax
import jax.numpy as jnp
from jax import lax
from jax.experimental import pallas as pl
from jax.experimental.pallas import tpu as pltpu
from jax.sharding import PartitionSpec as P

HEADS = 6
HD = 128
GROUP = 64

MATMUL_PRECISION = lax.Precision.HIGH


def mm(a, b):
    return lax.dot_general(
        a, b, (((1,), (0,)), ((), ())), precision=MATMUL_PRECISION,
        preferred_element_type=jnp.float32,
    )


def mm_nt(a, b):
    return lax.dot_general(
        a, b, (((1,), (1,)), ((), ())), precision=MATMUL_PRECISION,
        preferred_element_type=jnp.float32,
    )


def mm_tn(a, b):
    return lax.dot_general(
        a, b, (((0,), (0,)), ((), ())), precision=MATMUL_PRECISION,
        preferred_element_type=jnp.float32,
    )


def unit_normed(x):
    return x * lax.rsqrt(jnp.sum(x * x, -1, keepdims=True) + 1e-06)


def bmm(a, b):
    return lax.dot_general(
        a, b, (((2,), (1,)), ((0,), (0,))), precision=MATMUL_PRECISION,
        preferred_element_type=jnp.float32,
    )


def bmm_nt(a, b):
    return lax.dot_general(
        a, b, (((2,), (2,)), ((0,), (0,))), precision=MATMUL_PRECISION,
        preferred_element_type=jnp.float32,
    )


def delta_kernel(count, head_ref, mine_ref, feats_ref, *refs):
    slots = (len(refs) - 9) // 4
    weight_refs = refs[: 3 * slots]
    bw_ref, bias_ref = refs[3 * slots], refs[3 * slots + 1]
    gain_refs = refs[3 * slots + 2 : 4 * slots + 2]
    out_ref, qkv_ref, k_ref, w_ref, u_ref, p_ref, state_ref = refs[4 * slots + 2 :]
    frames = feats_ref.shape[1]
    chunks = frames // GROUP
    width = slots * HD

    full = feats_ref[...].T
    qkv_ref[...] = jnp.dot(
        full, jnp.concatenate([ref[...] for ref in weight_refs], axis=1),
        preferred_element_type=jnp.float32,
    ).astype(qkv_ref.dtype)
    logits = lax.dot_general(
        full, bw_ref[...], (((1,), (1,)), ((), ())), preferred_element_type=jnp.float32
    ) + bias_ref[...]
    beta_all = 1.0 / (1.0 + jnp.exp(-logits))
    lane = lax.broadcasted_iota(jnp.int32, beta_all.shape, 1)

    row = lax.broadcasted_iota(jnp.int32, (chunks, GROUP, GROUP), 1)
    col = lax.broadcasted_iota(jnp.int32, (chunks, GROUP, GROUP), 2)
    eye = jnp.where(row == col, 1.0, 0.0).astype(jnp.float32)

    pairs = chunks // 2
    for h in range(slots):
        query = unit_normed(qkv_ref[:, pl.ds(h * HD, HD)].astype(jnp.float32))
        keys = unit_normed(qkv_ref[:, pl.ds(width + h * HD, HD)].astype(jnp.float32))
        values = qkv_ref[:, pl.ds(2 * width + h * HD, HD)].astype(jnp.float32)
        rates = jnp.sum(jnp.where(lane == head_ref[h], beta_all, 0.0), -1, keepdims=True)
        weighted = (keys * rates).reshape(chunks, GROUP, HD)
        scaled = (values * rates).reshape(chunks, GROUP, HD)
        query = query.reshape(chunks, GROUP, HD)
        keys = keys.reshape(chunks, GROUP, HD)
        gram = bmm_nt(weighted, keys)
        negated = jnp.where(row > col, -gram, 0.0)
        inverse = eye + negated
        power = negated
        for level in range(5):
            power = bmm(power, power)
            inverse = inverse + bmm(inverse, power)
        wfac = bmm(inverse, weighted).reshape(pairs, 2, GROUP, HD)
        ufac = bmm(inverse, scaled).reshape(pairs, 2, GROUP, HD)
        scores = jnp.where(row >= col, bmm_nt(query, keys), 0.0).reshape(pairs, 2, GROUP, GROUP)
        query = query.reshape(pairs, 2, GROUP, HD)
        keys = keys.reshape(pairs, 2, GROUP, HD)
        w1, w2 = wfac[:, 0], wfac[:, 1]
        u1, u2 = ufac[:, 0], ufac[:, 1]
        k1 = keys[:, 0]
        q2 = query[:, 1]
        carry = bmm_nt(w2, k1)
        cross = bmm_nt(q2, k1)
        w_ref[h] = jnp.concatenate([w1, w2 - bmm(carry, w1), query[:, 0], q2], axis=1)
        u_ref[h] = jnp.concatenate([u1, u2 - bmm(carry, u1)], axis=1)
        k_ref[h] = jnp.swapaxes(keys.reshape(pairs, 2 * GROUP, HD), 1, 2)
        zero = jnp.zeros_like(cross)
        p_ref[h] = jnp.concatenate(
            [
                jnp.concatenate([scores[:, 0], zero], axis=2),
                jnp.concatenate([cross, scores[:, 1]], axis=2),
            ],
            axis=1,
        )

    state_ref[...] = jnp.zeros_like(state_ref)
    span = 2 * GROUP

    def step(c, carry):
        block = frames // count
        owner = ((c * span) // block - mine_ref[0] + count) % count
        place = pl.ds(pl.multiple_of(owner * block + (c * span) % block, span), span)
        for h in range(slots):
            state = state_ref[h]
            both = mm(w_ref[h, c], state)
            residual = u_ref[h, c] - both[:span]
            state_ref[h] = state + mm(k_ref[h, c], residual)
            output = both[span:] + mm(p_ref[h, c], residual)
            power_mean = jnp.mean(output * output, -1, keepdims=True) + 1e-06
            out_ref[place, pl.ds(h * HD, HD)] = (output * lax.rsqrt(power_mean) * gain_refs[h][...]).astype(
                out_ref.dtype
            )
        return carry

    lax.fori_loop(0, pairs, step, 0, unroll=pairs <= 8)


def delta_layer(heads, mine, full, qkv_weight, beta_weight, beta_bias, out_gain, count):
    channels, frames = full.shape
    slots = heads.shape[0]
    whole = lambda shape: pl.BlockSpec(shape, lambda i, head, mine: (0,) * len(shape))
    weight_specs = [
        pl.BlockSpec((channels, HD), lambda i, head, mine, p=p, j=j: (0, p * HEADS + head[j]))
        for p in range(3)
        for j in range(slots)
    ]
    gain_specs = [
        pl.BlockSpec((HD,), lambda i, head, mine, j=j: (head[j],)) for j in range(slots)
    ]
    grid_spec = pltpu.PrefetchScalarGridSpec(
        num_scalar_prefetch=2,
        grid=(1,),
        in_specs=[whole((channels, frames))]
        + weight_specs
        + [whole((HEADS, channels)), whole((1, HEADS))]
        + gain_specs,
        out_specs=whole((frames, slots * HD)),
        scratch_shapes=[
            pltpu.VMEM((frames, 3 * slots * HD), jnp.bfloat16),
            pltpu.VMEM((slots, frames // (2 * GROUP), HD, 2 * GROUP), jnp.float32),
            pltpu.VMEM((slots, frames // (2 * GROUP), 4 * GROUP, HD), jnp.float32),
            pltpu.VMEM((slots, frames // (2 * GROUP), 2 * GROUP, HD), jnp.float32),
            pltpu.VMEM((slots, frames // (2 * GROUP), 2 * GROUP, 2 * GROUP), jnp.float32),
            pltpu.VMEM((slots, HD, HD), jnp.float32),
        ],
    )
    gains = out_gain
    return pl.pallas_call(
        functools.partial(delta_kernel, count),
        out_shape=jax.ShapeDtypeStruct((frames, slots * HD), jnp.bfloat16),
        grid_spec=grid_spec,
    )(
        heads, mine, full, *([qkv_weight] * (3 * slots)), beta_weight.T, beta_bias.reshape(1, HEADS),
        *([gains] * slots),
    )


def body(feats, qkv_weight, beta_weight, beta_bias, out_gain):
    count = lax.axis_size("seq")
    mine = lax.axis_index("seq")
    slots = -(-HEADS // count)
    heads = jnp.minimum(mine * slots + jnp.arange(slots, dtype=jnp.int32), HEADS - 1)
    full = lax.all_gather(feats, "seq", axis=0, tiled=True)
    mixed = delta_layer(
        heads, mine.astype(jnp.int32).reshape(1), full, qkv_weight, beta_weight, beta_bias,
        out_gain, count,
    )
    frames = mixed.shape[0]
    rows = frames // count
    blocks = mixed.reshape(count, rows, slots * HD)
    got = [blocks[0]]
    for d in range(1, count):
        got.append(lax.ppermute(blocks[d], "seq", [(s, (s + d) % count) for s in range(count)]))
    needed = -(-HEADS // slots)
    placed = []
    for k in range(needed):
        pick = got[0]
        for d in range(1, count):
            pick = jnp.where((mine - d) % count == k, got[d], pick)
        placed.append(pick)
    return jnp.concatenate(placed, axis=1)[:, : HEADS * HD]


def solution(mesh):
    placed = (P("seq", "batch"), P(), P(), P(), P())
    return jax.shard_map(
        body, mesh=mesh, in_specs=placed, out_specs=P(("batch", "seq"), None), check_vma=False
    )
```

```python
import functools

import jax
import jax.numpy as jnp
from jax import lax
from jax.experimental import pallas as pl
from jax.experimental.pallas import tpu as pltpu
from jax.sharding import PartitionSpec as P

HEADS = 6
HD = 128
GROUP = 64

MATMUL_PRECISION = lax.Precision.HIGH


def mm(a, b):
    return lax.dot_general(
        a, b, (((1,), (0,)), ((), ())), precision=MATMUL_PRECISION,
        preferred_element_type=jnp.float32,
    )


def mm_nt(a, b):
    return lax.dot_general(
        a, b, (((1,), (1,)), ((), ())), precision=MATMUL_PRECISION,
        preferred_element_type=jnp.float32,
    )


def mm_tn(a, b):
    return lax.dot_general(
        a, b, (((0,), (0,)), ((), ())), precision=MATMUL_PRECISION,
        preferred_element_type=jnp.float32,
    )


def unit_normed(x):
    return x * lax.rsqrt(jnp.sum(x * x, -1, keepdims=True) + 1e-06)


def bmm(a, b):
    return lax.dot_general(
        a, b, (((2,), (1,)), ((0,), (0,))), precision=MATMUL_PRECISION,
        preferred_element_type=jnp.float32,
    )


def bmm_nt(a, b):
    return lax.dot_general(
        a, b, (((2,), (2,)), ((0,), (0,))), precision=MATMUL_PRECISION,
        preferred_element_type=jnp.float32,
    )


def delta_kernel(count, head_ref, mine_ref, feats_ref, *refs):
    slots = (len(refs) - 9) // 4
    weight_refs = refs[: 3 * slots]
    bw_ref, bias_ref = refs[3 * slots], refs[3 * slots + 1]
    gain_refs = refs[3 * slots + 2 : 4 * slots + 2]
    out_ref, qkv_ref, k_ref, w_ref, u_ref, p_ref, state_ref = refs[4 * slots + 2 :]
    frames = feats_ref.shape[1]
    chunks = frames // GROUP
    width = slots * HD

    full = feats_ref[...].T
    qkv_ref[...] = jnp.dot(
        full, jnp.concatenate([ref[...] for ref in weight_refs], axis=1),
        preferred_element_type=jnp.float32,
    ).astype(qkv_ref.dtype)
    logits = lax.dot_general(
        full, bw_ref[...], (((1,), (1,)), ((), ())), preferred_element_type=jnp.float32
    ) + bias_ref[...]
    beta_all = 1.0 / (1.0 + jnp.exp(-logits))
    lane = lax.broadcasted_iota(jnp.int32, beta_all.shape, 1)

    row = lax.broadcasted_iota(jnp.int32, (chunks, GROUP, GROUP), 1)
    col = lax.broadcasted_iota(jnp.int32, (chunks, GROUP, GROUP), 2)
    eye = jnp.where(row == col, 1.0, 0.0).astype(jnp.float32)

    pairs = chunks // 2
    for h in range(slots):
        query = unit_normed(qkv_ref[:, pl.ds(h * HD, HD)].astype(jnp.float32))
        keys = unit_normed(qkv_ref[:, pl.ds(width + h * HD, HD)].astype(jnp.float32))
        values = qkv_ref[:, pl.ds(2 * width + h * HD, HD)].astype(jnp.float32)
        rates = jnp.sum(jnp.where(lane == head_ref[h], beta_all, 0.0), -1, keepdims=True)
        weighted = (keys * rates).reshape(chunks, GROUP, HD)
        scaled = (values * rates).reshape(chunks, GROUP, HD)
        query = query.reshape(chunks, GROUP, HD)
        keys = keys.reshape(chunks, GROUP, HD)
        gram = bmm_nt(weighted, keys)
        negated = jnp.where(row > col, -gram, 0.0)
        inverse = eye + negated
        power = negated
        for level in range(5):
            power = bmm(power, power)
            inverse = inverse + bmm(inverse, power)
        wfac = bmm(inverse, weighted).reshape(pairs, 2, GROUP, HD)
        ufac = bmm(inverse, scaled).reshape(pairs, 2, GROUP, HD)
        scores = jnp.where(row >= col, bmm_nt(query, keys), 0.0).reshape(pairs, 2, GROUP, GROUP)
        query = query.reshape(pairs, 2, GROUP, HD)
        keys = keys.reshape(pairs, 2, GROUP, HD)
        w1, w2 = wfac[:, 0], wfac[:, 1]
        u1, u2 = ufac[:, 0], ufac[:, 1]
        k1 = keys[:, 0]
        q2 = query[:, 1]
        carry = bmm_nt(w2, k1)
        cross = bmm_nt(q2, k1)
        wp = jnp.concatenate([w1, w2 - bmm(carry, w1)], axis=1)
        up = jnp.concatenate([u1, u2 - bmm(carry, u1)], axis=1)
        kp = keys.reshape(pairs, 2 * GROUP, HD)
        qp = query.reshape(pairs, 2 * GROUP, HD)
        zero = jnp.zeros_like(cross)
        pp = jnp.concatenate(
            [
                jnp.concatenate([scores[:, 0], zero], axis=2),
                jnp.concatenate([cross, scores[:, 1]], axis=2),
            ],
            axis=1,
        )
        quads = pairs // 2
        wp = wp.reshape(quads, 2, 2 * GROUP, HD)
        up = up.reshape(quads, 2, 2 * GROUP, HD)
        kp = kp.reshape(quads, 2, 2 * GROUP, HD)
        qp = qp.reshape(quads, 2, 2 * GROUP, HD)
        pp = pp.reshape(quads, 2, 2 * GROUP, 2 * GROUP)
        carry2 = bmm_nt(wp[:, 1], kp[:, 0])
        cross2 = bmm_nt(qp[:, 1], kp[:, 0])
        w_ref[h] = jnp.concatenate(
            [wp[:, 0], wp[:, 1] - bmm(carry2, wp[:, 0]), qp[:, 0], qp[:, 1]], axis=1
        )
        u_ref[h] = jnp.concatenate([up[:, 0], up[:, 1] - bmm(carry2, up[:, 0])], axis=1)
        k_ref[h] = jnp.swapaxes(kp.reshape(quads, 4 * GROUP, HD), 1, 2)
        zero2 = jnp.zeros_like(cross2)
        p_ref[h] = jnp.concatenate(
            [
                jnp.concatenate([pp[:, 0], zero2], axis=2),
                jnp.concatenate([cross2, pp[:, 1]], axis=2),
            ],
            axis=1,
        )

    state_ref[...] = jnp.zeros_like(state_ref)
    span = 4 * GROUP
    piece = 2 * GROUP

    def step(c, carry):
        block = frames // count
        for h in range(slots):
            state = state_ref[h]
            both = mm(w_ref[h, c], state)
            residual = u_ref[h, c] - both[:span]
            state_ref[h] = state + mm(k_ref[h, c], residual)
            output = both[span:] + mm(p_ref[h, c], residual)
            power_mean = jnp.mean(output * output, -1, keepdims=True) + 1e-06
            mixed = (output * lax.rsqrt(power_mean) * gain_refs[h][...]).astype(out_ref.dtype)
            for e in range(span // piece):
                first = c * span + e * piece
                owner = (first // block - mine_ref[0] + count) % count
                place = pl.ds(pl.multiple_of(owner * block + first % block, piece), piece)
                out_ref[place, pl.ds(h * HD, HD)] = mixed[e * piece : (e + 1) * piece]
        return carry

    lax.fori_loop(0, chunks // 4, step, 0, unroll=chunks <= 16)


def delta_layer(heads, mine, full, qkv_weight, beta_weight, beta_bias, out_gain, count):
    channels, frames = full.shape
    slots = heads.shape[0]
    whole = lambda shape: pl.BlockSpec(shape, lambda i, head, mine: (0,) * len(shape))
    weight_specs = [
        pl.BlockSpec((channels, HD), lambda i, head, mine, p=p, j=j: (0, p * HEADS + head[j]))
        for p in range(3)
        for j in range(slots)
    ]
    gain_specs = [
        pl.BlockSpec((HD,), lambda i, head, mine, j=j: (head[j],)) for j in range(slots)
    ]
    grid_spec = pltpu.PrefetchScalarGridSpec(
        num_scalar_prefetch=2,
        grid=(1,),
        in_specs=[whole((channels, frames))]
        + weight_specs
        + [whole((HEADS, channels)), whole((1, HEADS))]
        + gain_specs,
        out_specs=whole((frames, slots * HD)),
        scratch_shapes=[
            pltpu.VMEM((frames, 3 * slots * HD), jnp.bfloat16),
            pltpu.VMEM((slots, frames // (4 * GROUP), HD, 4 * GROUP), jnp.float32),
            pltpu.VMEM((slots, frames // (4 * GROUP), 8 * GROUP, HD), jnp.float32),
            pltpu.VMEM((slots, frames // (4 * GROUP), 4 * GROUP, HD), jnp.float32),
            pltpu.VMEM((slots, frames // (4 * GROUP), 4 * GROUP, 4 * GROUP), jnp.float32),
            pltpu.VMEM((slots, HD, HD), jnp.float32),
        ],
    )
    gains = out_gain
    return pl.pallas_call(
        functools.partial(delta_kernel, count),
        out_shape=jax.ShapeDtypeStruct((frames, slots * HD), jnp.bfloat16),
        grid_spec=grid_spec,
    )(
        heads, mine, full, *([qkv_weight] * (3 * slots)), beta_weight.T, beta_bias.reshape(1, HEADS),
        *([gains] * slots),
    )


def body(feats, qkv_weight, beta_weight, beta_bias, out_gain):
    count = lax.axis_size("seq")
    mine = lax.axis_index("seq")
    slots = -(-HEADS // count)
    heads = jnp.minimum(mine * slots + jnp.arange(slots, dtype=jnp.int32), HEADS - 1)
    full = lax.all_gather(feats, "seq", axis=0, tiled=True)
    mixed = delta_layer(
        heads, mine.astype(jnp.int32).reshape(1), full, qkv_weight, beta_weight, beta_bias,
        out_gain, count,
    )
    frames = mixed.shape[0]
    rows = frames // count
    blocks = mixed.reshape(count, rows, slots * HD)
    got = [blocks[0]]
    for d in range(1, count):
        got.append(lax.ppermute(blocks[d], "seq", [(s, (s + d) % count) for s in range(count)]))
    needed = -(-HEADS // slots)
    placed = []
    for k in range(needed):
        pick = got[0]
        for d in range(1, count):
            pick = jnp.where((mine - d) % count == k, got[d], pick)
        placed.append(pick)
    return jnp.concatenate(placed, axis=1)[:, : HEADS * HD]


def solution(mesh):
    placed = (P("seq", "batch"), P(), P(), P(), P())
    return jax.shard_map(
        body, mesh=mesh, in_specs=placed, out_specs=P(("batch", "seq"), None), check_vma=False
    )
```

```python
import functools

import jax
import jax.numpy as jnp
from jax import lax
from jax.experimental import pallas as pl
from jax.experimental.pallas import tpu as pltpu
from jax.sharding import PartitionSpec as P

HEADS = 6
HD = 128
GROUP = 64

MATMUL_PRECISION = lax.Precision.HIGH


def mm(a, b):
    return lax.dot_general(
        a, b, (((1,), (0,)), ((), ())), precision=MATMUL_PRECISION,
        preferred_element_type=jnp.float32,
    )


def mm_nt(a, b):
    return lax.dot_general(
        a, b, (((1,), (1,)), ((), ())), precision=MATMUL_PRECISION,
        preferred_element_type=jnp.float32,
    )


def mm_tn(a, b):
    return lax.dot_general(
        a, b, (((0,), (0,)), ((), ())), precision=MATMUL_PRECISION,
        preferred_element_type=jnp.float32,
    )


def unit_normed(x):
    return x * lax.rsqrt(jnp.sum(x * x, -1, keepdims=True) + 1e-06)


def bmm(a, b):
    return lax.dot_general(
        a, b, (((2,), (1,)), ((0,), (0,))), precision=MATMUL_PRECISION,
        preferred_element_type=jnp.float32,
    )


def bmm_nt(a, b):
    return lax.dot_general(
        a, b, (((2,), (2,)), ((0,), (0,))), precision=MATMUL_PRECISION,
        preferred_element_type=jnp.float32,
    )


def delta_kernel(count, slots_arg, mine_ref, feats_ref, *refs):
    slots = (len(refs) - 9) // 4
    weight_refs = refs[: 3 * slots]
    bw_ref, bias_ref = refs[3 * slots], refs[3 * slots + 1]
    gain_refs = refs[3 * slots + 2 : 4 * slots + 2]
    out_ref, qkv_ref, k_ref, w_ref, u_ref, p_ref, state_ref = refs[4 * slots + 2 :]
    frames = feats_ref.shape[1]
    chunks = frames // GROUP
    width = slots * HD

    full = feats_ref[...].T
    qkv_ref[...] = jnp.dot(
        full, jnp.concatenate([ref[...] for ref in weight_refs], axis=1),
        preferred_element_type=jnp.float32,
    ).astype(qkv_ref.dtype)
    logits = lax.dot_general(
        full, bw_ref[...], (((1,), (1,)), ((), ())), preferred_element_type=jnp.float32
    ) + bias_ref[...]
    beta_all = 1.0 / (1.0 + jnp.exp(-logits))
    lane = lax.broadcasted_iota(jnp.int32, beta_all.shape, 1)

    row = lax.broadcasted_iota(jnp.int32, (chunks, GROUP, GROUP), 1)
    col = lax.broadcasted_iota(jnp.int32, (chunks, GROUP, GROUP), 2)
    eye = jnp.where(row == col, 1.0, 0.0).astype(jnp.float32)

    pairs = chunks // 2
    for h in range(slots):
        query = unit_normed(qkv_ref[:, pl.ds(h * HD, HD)].astype(jnp.float32))
        keys = unit_normed(qkv_ref[:, pl.ds(width + h * HD, HD)].astype(jnp.float32))
        values = qkv_ref[:, pl.ds(2 * width + h * HD, HD)].astype(jnp.float32)
        head = jnp.minimum(mine_ref[0] * slots + h, HEADS - 1)
        rates = jnp.sum(jnp.where(lane == head, beta_all, 0.0), -1, keepdims=True)
        weighted = (keys * rates).reshape(chunks, GROUP, HD)
        scaled = (values * rates).reshape(chunks, GROUP, HD)
        query = query.reshape(chunks, GROUP, HD)
        keys = keys.reshape(chunks, GROUP, HD)
        gram = bmm_nt(weighted, keys)
        negated = jnp.where(row > col, -gram, 0.0)
        inverse = eye + negated
        power = negated
        for level in range(5):
            power = bmm(power, power)
            inverse = inverse + bmm(inverse, power)
        wfac = bmm(inverse, weighted).reshape(pairs, 2, GROUP, HD)
        ufac = bmm(inverse, scaled).reshape(pairs, 2, GROUP, HD)
        scores = jnp.where(row >= col, bmm_nt(query, keys), 0.0).reshape(pairs, 2, GROUP, GROUP)
        query = query.reshape(pairs, 2, GROUP, HD)
        keys = keys.reshape(pairs, 2, GROUP, HD)
        w1, w2 = wfac[:, 0], wfac[:, 1]
        u1, u2 = ufac[:, 0], ufac[:, 1]
        k1 = keys[:, 0]
        q2 = query[:, 1]
        carry = bmm_nt(w2, k1)
        cross = bmm_nt(q2, k1)
        w_ref[h] = jnp.concatenate([w1, w2 - bmm(carry, w1), query[:, 0], q2], axis=1)
        u_ref[h] = jnp.concatenate([u1, u2 - bmm(carry, u1)], axis=1)
        k_ref[h] = jnp.swapaxes(keys.reshape(pairs, 2 * GROUP, HD), 1, 2)
        zero = jnp.zeros_like(cross)
        p_ref[h] = jnp.concatenate(
            [
                jnp.concatenate([scores[:, 0], zero], axis=2),
                jnp.concatenate([cross, scores[:, 1]], axis=2),
            ],
            axis=1,
        )

    state_ref[...] = jnp.zeros_like(state_ref)
    span = 2 * GROUP

    def step(c, carry):
        block = frames // count
        owner = ((c * span) // block - mine_ref[0] + count) % count
        place = pl.ds(pl.multiple_of(owner * block + (c * span) % block, span), span)
        for h in range(slots):
            state = state_ref[h]
            both = mm(w_ref[h, c], state)
            residual = u_ref[h, c] - both[:span]
            state_ref[h] = state + mm(k_ref[h, c], residual)
            output = both[span:] + mm(p_ref[h, c], residual)
            power_mean = jnp.mean(output * output, -1, keepdims=True) + 1e-06
            out_ref[place, pl.ds(h * HD, HD)] = (output * lax.rsqrt(power_mean) * gain_refs[h][...]).astype(
                out_ref.dtype
            )
        return carry

    lax.fori_loop(0, pairs, step, 0, unroll=pairs <= 8)


def delta_layer(slots, mine, full, qkv_weight, beta_weight, beta_bias, out_gain, count):
    channels, frames = full.shape
    pick = lambda mine, j: jnp.minimum(mine[0] * slots + j, HEADS - 1)
    whole = lambda shape: pl.BlockSpec(shape, lambda i, mine: (0,) * len(shape))
    weight_specs = [
        pl.BlockSpec((channels, HD), lambda i, mine, p=p, j=j: (0, p * HEADS + pick(mine, j)))
        for p in range(3)
        for j in range(slots)
    ]
    gain_specs = [
        pl.BlockSpec((HD,), lambda i, mine, j=j: (pick(mine, j),)) for j in range(slots)
    ]
    grid_spec = pltpu.PrefetchScalarGridSpec(
        num_scalar_prefetch=1,
        grid=(1,),
        in_specs=[whole((channels, frames))]
        + weight_specs
        + [whole((HEADS, channels)), whole((1, HEADS))]
        + gain_specs,
        out_specs=whole((frames, slots * HD)),
        scratch_shapes=[
            pltpu.VMEM((frames, 3 * slots * HD), jnp.bfloat16),
            pltpu.VMEM((slots, frames // (2 * GROUP), HD, 2 * GROUP), jnp.float32),
            pltpu.VMEM((slots, frames // (2 * GROUP), 4 * GROUP, HD), jnp.float32),
            pltpu.VMEM((slots, frames // (2 * GROUP), 2 * GROUP, HD), jnp.float32),
            pltpu.VMEM((slots, frames // (2 * GROUP), 2 * GROUP, 2 * GROUP), jnp.float32),
            pltpu.VMEM((slots, HD, HD), jnp.float32),
        ],
    )
    gains = out_gain
    return pl.pallas_call(
        functools.partial(delta_kernel, count, slots),
        out_shape=jax.ShapeDtypeStruct((frames, slots * HD), jnp.bfloat16),
        grid_spec=grid_spec,
    )(
        mine, full, *([qkv_weight] * (3 * slots)), beta_weight.T, beta_bias.reshape(1, HEADS),
        *([gains] * slots),
    )


def body(feats, qkv_weight, beta_weight, beta_bias, out_gain):
    count = lax.axis_size("seq")
    mine = lax.axis_index("seq")
    slots = -(-HEADS // count)
    full = lax.all_gather(feats, "seq", axis=0, tiled=True)
    mixed = delta_layer(
        slots, mine.astype(jnp.int32).reshape(1), full, qkv_weight, beta_weight, beta_bias,
        out_gain, count,
    )
    frames = mixed.shape[0]
    rows = frames // count
    blocks = mixed.reshape(count, rows, slots * HD)
    got = [blocks[0]]
    for d in range(1, count):
        got.append(lax.ppermute(blocks[d], "seq", [(s, (s + d) % count) for s in range(count)]))
    needed = -(-HEADS // slots)
    placed = []
    for k in range(needed):
        pick = got[0]
        for d in range(1, count):
            pick = jnp.where((mine - d) % count == k, got[d], pick)
        placed.append(pick)
    return jnp.concatenate(placed, axis=1)[:, : HEADS * HD]


def solution(mesh):
    placed = (P("seq", "batch"), P(), P(), P(), P())
    return jax.shard_map(
        body, mesh=mesh, in_specs=placed, out_specs=P(("batch", "seq"), None), check_vma=False
    )
```

```python
import functools

import jax
import jax.numpy as jnp
from jax import lax
from jax.experimental import pallas as pl
from jax.experimental.pallas import tpu as pltpu
from jax.sharding import PartitionSpec as P

HEADS = 6
HD = 128
GROUP = 64

MATMUL_PRECISION = lax.Precision.HIGH


def mm(a, b):
    return lax.dot_general(
        a, b, (((1,), (0,)), ((), ())), precision=MATMUL_PRECISION,
        preferred_element_type=jnp.float32,
    )


def mm_nt(a, b):
    return lax.dot_general(
        a, b, (((1,), (1,)), ((), ())), precision=MATMUL_PRECISION,
        preferred_element_type=jnp.float32,
    )


def mm_tn(a, b):
    return lax.dot_general(
        a, b, (((0,), (0,)), ((), ())), precision=MATMUL_PRECISION,
        preferred_element_type=jnp.float32,
    )


def unit_normed(x):
    return x * lax.rsqrt(jnp.sum(x * x, -1, keepdims=True) + 1e-06)


def bmm(a, b):
    return lax.dot_general(
        a, b, (((2,), (1,)), ((0,), (0,))), precision=MATMUL_PRECISION,
        preferred_element_type=jnp.float32,
    )


def bmm_nt(a, b):
    return lax.dot_general(
        a, b, (((2,), (2,)), ((0,), (0,))), precision=MATMUL_PRECISION,
        preferred_element_type=jnp.float32,
    )


def delta_kernel(count, slots_arg, mine_ref, feats_ref, *refs):
    slots = (len(refs) - 9) // 4
    weight_refs = refs[: 3 * slots]
    bw_ref, bias_ref = refs[3 * slots], refs[3 * slots + 1]
    gain_refs = refs[3 * slots + 2 : 4 * slots + 2]
    out_ref, qkv_ref, k_ref, w_ref, u_ref, p_ref, state_ref = refs[4 * slots + 2 :]
    frames = feats_ref.shape[1]
    chunks = frames // GROUP
    width = slots * HD

    full = feats_ref[...].T
    qkv_ref[...] = jnp.dot(
        full, jnp.concatenate([ref[...] for ref in weight_refs], axis=1),
        preferred_element_type=jnp.float32,
    ).astype(qkv_ref.dtype)
    logits = lax.dot_general(
        full, bw_ref[...], (((1,), (1,)), ((), ())), preferred_element_type=jnp.float32
    ) + bias_ref[...]
    beta_all = 1.0 / (1.0 + jnp.exp(-logits))
    lane = lax.broadcasted_iota(jnp.int32, beta_all.shape, 1)

    row = lax.broadcasted_iota(jnp.int32, (chunks, GROUP, GROUP), 1)
    col = lax.broadcasted_iota(jnp.int32, (chunks, GROUP, GROUP), 2)
    eye = jnp.where(row == col, 1.0, 0.0).astype(jnp.float32)

    pairs = chunks // 2
    for h in range(slots):
        query = unit_normed(qkv_ref[:, pl.ds(h * HD, HD)].astype(jnp.float32))
        keys = unit_normed(qkv_ref[:, pl.ds(width + h * HD, HD)].astype(jnp.float32))
        values = qkv_ref[:, pl.ds(2 * width + h * HD, HD)].astype(jnp.float32)
        head = jnp.minimum(mine_ref[0] * slots + h, HEADS - 1)
        rates = jnp.sum(jnp.where(lane == head, beta_all, 0.0), -1, keepdims=True)
        weighted = (keys * rates).reshape(chunks, GROUP, HD)
        scaled = (values * rates).reshape(chunks, GROUP, HD)
        query = query.reshape(chunks, GROUP, HD)
        keys = keys.reshape(chunks, GROUP, HD)
        gram = bmm_nt(weighted, keys)
        negated = jnp.where(row > col, -gram, 0.0)
        inverse = eye + negated
        power = negated
        for level in range(5):
            power = bmm(power, power)
            inverse = inverse + bmm(inverse, power)
        wfac = bmm(inverse, weighted).reshape(pairs, 2, GROUP, HD)
        ufac = bmm(inverse, scaled).reshape(pairs, 2, GROUP, HD)
        scores = jnp.where(row >= col, bmm_nt(query, keys), 0.0).reshape(pairs, 2, GROUP, GROUP)
        query = query.reshape(pairs, 2, GROUP, HD)
        keys = keys.reshape(pairs, 2, GROUP, HD)
        w1, w2 = wfac[:, 0], wfac[:, 1]
        u1, u2 = ufac[:, 0], ufac[:, 1]
        k1 = keys[:, 0]
        q2 = query[:, 1]
        carry = bmm_nt(w2, k1)
        cross = bmm_nt(q2, k1)
        w_ref[h] = jnp.concatenate([w1, w2 - bmm(carry, w1), query[:, 0], q2], axis=1)
        u_ref[h] = jnp.concatenate([u1, u2 - bmm(carry, u1)], axis=1)
        k_ref[h] = jnp.swapaxes(keys.reshape(pairs, 2 * GROUP, HD), 1, 2)
        zero = jnp.zeros_like(cross)
        p_ref[h] = jnp.concatenate(
            [
                jnp.concatenate([scores[:, 0], zero], axis=2),
                jnp.concatenate([cross, scores[:, 1]], axis=2),
            ],
            axis=1,
        )

    state_ref[...] = jnp.zeros_like(state_ref)
    span = 2 * GROUP

    def step(c, carry):
        block = frames // count
        owner = ((c * span) // block - mine_ref[0] + count) % count
        place = pl.ds(pl.multiple_of(owner * block + (c * span) % block, span), span)
        for h in range(slots):
            state = state_ref[h]
            both = mm(w_ref[h, c], state)
            residual = u_ref[h, c] - both[:span]
            state_ref[h] = state + mm(k_ref[h, c], residual)
            output = both[span:] + jnp.dot(
                p_ref[h, c], residual, preferred_element_type=jnp.float32
            )
            power_mean = jnp.mean(output * output, -1, keepdims=True) + 1e-06
            out_ref[place, pl.ds(h * HD, HD)] = (output * lax.rsqrt(power_mean) * gain_refs[h][...]).astype(
                out_ref.dtype
            )
        return carry

    lax.fori_loop(0, pairs, step, 0, unroll=pairs <= 8)


def delta_layer(slots, mine, full, qkv_weight, beta_weight, beta_bias, out_gain, count):
    channels, frames = full.shape
    pick = lambda mine, j: jnp.minimum(mine[0] * slots + j, HEADS - 1)
    whole = lambda shape: pl.BlockSpec(shape, lambda i, mine: (0,) * len(shape))
    weight_specs = [
        pl.BlockSpec((channels, HD), lambda i, mine, p=p, j=j: (0, p * HEADS + pick(mine, j)))
        for p in range(3)
        for j in range(slots)
    ]
    gain_specs = [
        pl.BlockSpec((HD,), lambda i, mine, j=j: (pick(mine, j),)) for j in range(slots)
    ]
    grid_spec = pltpu.PrefetchScalarGridSpec(
        num_scalar_prefetch=1,
        grid=(1,),
        in_specs=[whole((channels, frames))]
        + weight_specs
        + [whole((HEADS, channels)), whole((1, HEADS))]
        + gain_specs,
        out_specs=whole((frames, slots * HD)),
        scratch_shapes=[
            pltpu.VMEM((frames, 3 * slots * HD), jnp.bfloat16),
            pltpu.VMEM((slots, frames // (2 * GROUP), HD, 2 * GROUP), jnp.float32),
            pltpu.VMEM((slots, frames // (2 * GROUP), 4 * GROUP, HD), jnp.float32),
            pltpu.VMEM((slots, frames // (2 * GROUP), 2 * GROUP, HD), jnp.float32),
            pltpu.VMEM((slots, frames // (2 * GROUP), 2 * GROUP, 2 * GROUP), jnp.float32),
            pltpu.VMEM((slots, HD, HD), jnp.float32),
        ],
    )
    gains = out_gain
    return pl.pallas_call(
        functools.partial(delta_kernel, count, slots),
        out_shape=jax.ShapeDtypeStruct((frames, slots * HD), jnp.bfloat16),
        grid_spec=grid_spec,
    )(
        mine, full, *([qkv_weight] * (3 * slots)), beta_weight.T, beta_bias.reshape(1, HEADS),
        *([gains] * slots),
    )


def body(feats, qkv_weight, beta_weight, beta_bias, out_gain):
    count = lax.axis_size("seq")
    mine = lax.axis_index("seq")
    slots = -(-HEADS // count)
    full = lax.all_gather(feats, "seq", axis=0, tiled=True)
    mixed = delta_layer(
        slots, mine.astype(jnp.int32).reshape(1), full, qkv_weight, beta_weight, beta_bias,
        out_gain, count,
    )
    frames = mixed.shape[0]
    rows = frames // count
    blocks = mixed.reshape(count, rows, slots * HD)
    got = [blocks[0]]
    for d in range(1, count):
        got.append(lax.ppermute(blocks[d], "seq", [(s, (s + d) % count) for s in range(count)]))
    needed = -(-HEADS // slots)
    placed = []
    for k in range(needed):
        pick = got[0]
        for d in range(1, count):
            pick = jnp.where((mine - d) % count == k, got[d], pick)
        placed.append(pick)
    return jnp.concatenate(placed, axis=1)[:, : HEADS * HD]


def solution(mesh):
    placed = (P("seq", "batch"), P(), P(), P(), P())
    return jax.shard_map(
        body, mesh=mesh, in_specs=placed, out_specs=P(("batch", "seq"), None), check_vma=False
    )
```
